32 devices in a mesh: ctx: 8 (over z, x), tp: 4 (over y, core).
Axes of the slice: x: 2, y: 2, z: 4, core: 2. Of those that a mesh axis runs over, the one named last changes fastest.
Arguments:
- inner_input: bfloat16 [4096, 8192], P('ctx', 'tp'), may hold values from -6 to 6
- state_input: bfloat16 [4096, 2, 1024], P('ctx', None, 'tp'), may hold values from -6 to 6
- gate_input: bfloat16 [4096, 8192], P('ctx', 'tp'), may hold values from -40 to 40
- step_logits: float32 [4096, 128], P('ctx', 'tp'), may hold values from -20 to 1
- conv_inner: bfloat16 [4, 8192], P(None, 'tp'), may hold values from -3 to 3
- conv_states: bfloat16 [4, 2, 1024], P(None, None, 'tp'), may hold values from -3 to 3
- bias_inner: bfloat16 [8192], P('tp'), may hold values from -0.5 to 0.5
- bias_states: bfloat16 [2, 1024], P(None, 'tp'), may hold values from -0.5 to 0.5
- decay_log: float32 [128], P('tp'), may hold values from -0.7 to 0.7
- skip_gain: float32 [128], P('tp'), may hold values from 0.5 to 1.5
- norm_gain: bfloat16 [8192], P('tp'), may hold values from 0.5 to 1.5
- out_weight: bfloat16 [8192, 4096], P('tp'), may hold values from -0.0625 to 0.0625
Outputs:
- layer_out: bfloat16 [4096, 4096], P(('ctx', 'tp'))
The draws below stay inside these ranges and needn't reach their ends.
All inputs are finite; a program needn't handle non-finite values.
Results may differ from the reference program's by a relative error of at most 0.009.
Values may be sent and summed in bfloat16 or wider, within the bound.
No kernel may reach another device: no remote copies, remote signals or barrier semaphores. Data moves between devices by JAX's collectives and lax.ppermute only.
A program may use at most 128 MiB of HBM per device.

```python
import math
import jax
import jax.numpy as jnp
from jax import lax

SSM_HEAD_COUNT = 128
HEAD_DIM = 64
STATE = 128
GROUPS = 8
CONV = 4
OUT = 4096
TOK_DEV = 512
D_INNER = 8192
SEQUENCE_LENGTH = 4096
BLK = 512
N_TP = 4


def head_table(key):
    shared = jax.random.fold_in(key, 7)
    magnitude = jnp.exp(jax.random.uniform(jax.random.fold_in(shared, 1), (SSM_HEAD_COUNT,), jnp.float32, math.log(0.5), math.log(2.0)))
    slow_share = 0.5
    sluggish_heads = jax.random.uniform(jax.random.fold_in(shared, 2), (SSM_HEAD_COUNT,), jnp.float32) < slow_share
    return (magnitude, sluggish_heads)


def draw_decay_log(key, part):
    magnitude, sluggish_heads = head_table(key)
    return jnp.log(magnitude)


def draw_step_logits(key, part):
    magnitude, sluggish_heads = head_table(key)
    self_portion = jax.random.fold_in(key, 11)
    jitter = jax.random.uniform(jax.random.fold_in(self_portion, 1), (SEQUENCE_LENGTH, SSM_HEAD_COUNT), jnp.float32, 0.5, 1.5)
    block_level = jnp.exp(jax.random.uniform(jax.random.fold_in(self_portion, 2), (SEQUENCE_LENGTH // TOK_DEV, SSM_HEAD_COUNT), jnp.float32, math.log(0.5), math.log(2.0)))
    block_level = jnp.repeat(block_level, TOK_DEV, axis=0, total_repeat_length=SEQUENCE_LENGTH)
    fast_rate = jnp.exp(jax.random.uniform(jax.random.fold_in(self_portion, 3), (SSM_HEAD_COUNT,), jnp.float32, math.log(0.02), math.log(0.033)))
    baseline = jnp.where(sluggish_heads, 0.4 / SEQUENCE_LENGTH, fast_rate)
    rates_combined = baseline[None] * jitter * block_level
    locations = jax.random.randint(jax.random.fold_in(self_portion, 4), (2, SSM_HEAD_COUNT), 0, SEQUENCE_LENGTH)
    spike_mask = jnp.any(jnp.arange(SEQUENCE_LENGTH)[:, None, None] == locations[None], axis=1) & sluggish_heads[None]
    spike_rate = jax.random.uniform(jax.random.fold_in(self_portion, 5), (SEQUENCE_LENGTH, SSM_HEAD_COUNT), jnp.float32, 0.22, 0.5)
    rates_combined = jnp.where(spike_mask, spike_rate, rates_combined)
    step_size = rates_combined / magnitude[None]
    return jnp.log(jnp.expm1(step_size))


def draw_gate_input(key, part):
    self_portion = jax.random.fold_in(key, 23)
    baseline = jax.random.normal(jax.random.fold_in(self_portion, 1), (SEQUENCE_LENGTH, D_INNER), jnp.float32)
    row_scale = jnp.exp(jax.random.uniform(jax.random.fold_in(self_portion, 2), (SEQUENCE_LENGTH, 1), jnp.float32, math.log(0.5), math.log(5.0)))
    column_scale = jnp.exp(jax.random.uniform(jax.random.fold_in(self_portion, 3), (1, D_INNER), jnp.float32, math.log(0.5), math.log(5.0)))
    return jnp.clip(baseline * row_scale * column_scale, -40.0, 40.0).astype(jnp.bfloat16)


def block_levels(rng, extent, cuts, low, top_value):
    def one(dim, shards_of):
        steps = jax.random.uniform(jax.random.fold_in(jax.random.fold_in(rng, 6), dim), (shards_of,), jnp.float32, low / len(cuts), top_value / len(cuts))
        return jnp.repeat(jnp.exp(steps), extent[dim] // shards_of).reshape((-1,) + (1,) * (len(extent) - dim - 1))

    gain = one(*cuts[0])
    for cut in cuts[1:]:
        gain = gain * one(*cut)
    return gain


def bell_draw(key, shape, scale, limit, cuts=(), dtype=jnp.bfloat16):
    level = block_levels(key, shape, cuts, -0.22, 0.18) if cuts else 1.0
    drawn = jax.random.normal(key, shape, jnp.float32) * scale * level
    return jnp.minimum(jnp.maximum(drawn, -limit), limit).astype(dtype)


def setup_inputs(seed: int = 0) -> dict:
    seeds = jax.random.split(jax.random.key(seed), 13)
    return {
        "inner_input": bell_draw(seeds[0], (SEQUENCE_LENGTH, D_INNER), 1.0, 6.0, ((0, 8), (1, 4))),
        "state_input": bell_draw(seeds[1], (SEQUENCE_LENGTH, 2, GROUPS * STATE), 1.0, 6.0, ((0, 8), (2, 4))),
        "gate_input": draw_gate_input(jax.random.fold_in(seeds[12], 71), 0),
        "step_logits": draw_step_logits(jax.random.fold_in(seeds[12], 71), 0),
        "conv_inner": bell_draw(seeds[4], (CONV, D_INNER), CONV ** -0.5, 3.0, ((1, 4),)),
        "conv_states": bell_draw(seeds[5], (CONV, 2, GROUPS * STATE), CONV ** -0.5, 3.0, ((2, 4),)),
        "bias_inner": jnp.clip(jax.random.uniform(seeds[6], (D_INNER,), jnp.float32, -0.5, 0.5) * block_levels(seeds[6], (D_INNER,), ((0, 4),), -0.4, 0.0), -0.5, 0.5).astype(jnp.bfloat16),
        "bias_states": jnp.clip(jax.random.uniform(seeds[7], (2, GROUPS * STATE), jnp.float32, -0.5, 0.5) * block_levels(seeds[7], (2, GROUPS * STATE), ((1, 4),), -0.4, 0.0), -0.5, 0.5).astype(jnp.bfloat16),
        "decay_log": draw_decay_log(jax.random.fold_in(seeds[12], 71), 0),
        "skip_gain": jnp.clip(0.5 + 1.0 * jax.random.uniform(seeds[9], (SSM_HEAD_COUNT,), jnp.float32) ** block_levels(seeds[9], (SSM_HEAD_COUNT,), ((0, 4),), -0.2, 0.2), 0.5, 1.5),
        "norm_gain": jnp.clip(0.5 + 1.0 * jax.random.uniform(seeds[10], (D_INNER,), jnp.float32) ** block_levels(seeds[10], (D_INNER,), ((0, 4),), -0.2, 0.2), 0.5, 1.5).astype(jnp.bfloat16),
        "out_weight": bell_draw(seeds[11], (D_INNER, OUT), D_INNER ** -0.5, 0.0625, ((0, 4),)),
    }


epsilon = 1e-05

def conv_silu(padded, weight, offsets, row_count):
    summed = offsets.astype(jnp.float32)
    for k in range(CONV):
        summed = summed + weight[k].astype(jnp.float32) * padded[k:k + row_count].astype(jnp.float32)
    return lax.optimization_barrier(jax.nn.silu(summed).astype(jnp.bfloat16))

def block_step(state_now, inputs_block):
    inner_block, b_block, c_block, step_sizes, log_rates = inputs_block
    length = inner_block.shape[0]
    cumulative = jnp.cumsum(log_rates, axis=0)
    along = jnp.transpose(cumulative, (1, 2, 0))
    causal = lax.broadcasted_iota(jnp.int32, (length, length), 0) >= lax.broadcasted_iota(jnp.int32, (length, length), 1)
    decays = jnp.exp(jnp.where(causal, along[:, :, :, None] - along[:, :, None, :], -jnp.inf))
    b_wide = b_block.astype(jnp.float32)
    c_wide = c_block.astype(jnp.float32)
    scores = jnp.einsum('ign,jgn->gij', c_wide, b_wide)
    mixing = decays * scores[:, None] * jnp.transpose(step_sizes, (1, 2, 0))[:, :, None, :]
    mixing = lax.optimization_barrier(mixing.astype(jnp.bfloat16))
    inner_wide = inner_block.astype(jnp.float32)
    diagonal = jnp.einsum('ghij,jghp->ighp', mixing.astype(jnp.float32), inner_wide)
    carried = jnp.exp(cumulative)[..., None] * jnp.einsum('ign,ghpn->ighp', c_wide, state_now, precision=lax.Precision.HIGHEST)
    tail_weight = jnp.exp(cumulative[-1][None] - cumulative) * step_sizes
    weighted = lax.optimization_barrier((inner_wide * tail_weight[..., None]).astype(jnp.bfloat16))
    block_state = jnp.einsum('jghp,jgn->ghpn', weighted.astype(jnp.float32), b_wide)
    new_state = jnp.exp(cumulative[-1])[..., None, None] * state_now + block_state
    return (new_state, diagonal + carried)

def reference(inner_input, state_input, gate_input, step_logits, conv_inner, conv_states, bias_inner, bias_states, decay_log, skip_gain, norm_gain, out_weight):
    margin = CONV - 1
    inner_conv = conv_silu(jnp.concatenate([jnp.zeros((margin, D_INNER), jnp.bfloat16), inner_input], axis=0), conv_inner, bias_inner, SEQUENCE_LENGTH)
    state_conv = conv_silu(jnp.concatenate([jnp.zeros((margin, 2, GROUPS * STATE), jnp.bfloat16), state_input], axis=0), conv_states, bias_states, SEQUENCE_LENGTH)
    step_sizes = jax.nn.softplus(step_logits)
    log_rates = -step_sizes * jnp.exp(decay_log)[None]
    per_group = SSM_HEAD_COUNT // GROUPS
    blocks = SEQUENCE_LENGTH // BLK
    inputs_all = (inner_conv.reshape(blocks, BLK, GROUPS, per_group, HEAD_DIM), state_conv[:, 0].reshape(blocks, BLK, GROUPS, STATE), state_conv[:, 1].reshape(blocks, BLK, GROUPS, STATE), step_sizes.reshape(blocks, BLK, GROUPS, per_group), log_rates.reshape(blocks, BLK, GROUPS, per_group))
    start_state = jnp.zeros((GROUPS, per_group, HEAD_DIM, STATE), jnp.float32)
    _, outputs = lax.scan(block_step, start_state, inputs_all)
    mixed_heads = outputs.reshape(SEQUENCE_LENGTH, D_INNER) + jnp.repeat(skip_gain, HEAD_DIM)[None] * inner_conv.astype(jnp.float32)
    gated_out = mixed_heads * jax.nn.silu(gate_input.astype(jnp.float32))
    grouped = gated_out.reshape(SEQUENCE_LENGTH, GROUPS, D_INNER // GROUPS)
    normed = grouped * lax.rsqrt(lax.optimization_barrier(jnp.mean(grouped * grouped, axis=-1, keepdims=True)) + epsilon)
    normed = lax.optimization_barrier((normed.reshape(SEQUENCE_LENGTH, D_INNER) * norm_gain.astype(jnp.float32)).astype(jnp.bfloat16))
    width = D_INNER // N_TP
    running = jnp.zeros((SEQUENCE_LENGTH, OUT), jnp.float32)
    for k in range(N_TP):
        partial_sum = jnp.dot(normed[:, k * width:(k + 1) * width], out_weight[k * width:(k + 1) * width], preferred_element_type=jnp.float32)
        running = running + lax.optimization_barrier(partial_sum.astype(jnp.bfloat16)).astype(jnp.float32)
    return running.astype(jnp.bfloat16)
```

```python
import jax
import jax.numpy as jnp
from jax import lax
from jax.sharding import PartitionSpec as P

SSM_HEAD_COUNT = 128
HEAD_DIM = 64
STATE = 128
GROUPS = 8
CONV = 4
BLK = 512


epsilon = 1e-05


def shifted(value, axis, by):
    count = lax.axis_size(axis)
    pairs = [(i, i + by) for i in range(count) if 0 <= i + by < count]
    return lax.ppermute(value, axis, pairs)


def conv_silu(padded, weight, offsets, row_count):
    summed = offsets.astype(jnp.float32)
    for k in range(CONV):
        summed = summed + weight[k].astype(jnp.float32) * padded[k : k + row_count].astype(
            jnp.float32
        )
    return lax.optimization_barrier(jax.nn.silu(summed).astype(jnp.bfloat16))


def block_parts(inner_block, b_block, c_block, step_sizes, log_rates):
    length = inner_block.shape[0]
    cumulative = jnp.cumsum(log_rates, axis=0)
    along = jnp.transpose(cumulative, (1, 2, 0))
    causal = lax.broadcasted_iota(jnp.int32, (length, length), 0) >= lax.broadcasted_iota(
        jnp.int32, (length, length), 1
    )
    decays = jnp.exp(jnp.where(causal, along[:, :, :, None] - along[:, :, None, :], -jnp.inf))
    scores = jnp.einsum("ign,jgn->gij", c_block, b_block, preferred_element_type=jnp.float32)
    mixing = (
        decays * scores[:, None] * jnp.transpose(step_sizes, (1, 2, 0))[:, :, None, :]
    ).astype(jnp.bfloat16)
    diagonal = jnp.einsum(
        "ghij,jghp->ighp", mixing, inner_block, preferred_element_type=jnp.float32
    )
    tail_weight = jnp.exp(cumulative[-1][None] - cumulative) * step_sizes
    weighted = (inner_block * tail_weight[..., None]).astype(jnp.bfloat16)
    block_state = jnp.einsum(
        "jghp,jgn->ghpn", weighted, b_block, preferred_element_type=jnp.float32
    )
    return diagonal, cumulative, block_state


def apply_state(c_block, state, cumulative):
    return jnp.exp(cumulative)[..., None] * jnp.einsum(
        "ign,ghpn->ighp", c_block.astype(jnp.float32), state, precision=lax.Precision.HIGHEST
    )


def block_local(carried_in, inputs_block):
    local_state, entry_total = carried_in
    inner_block, b_block, c_block, step_sizes, log_rates = inputs_block
    diagonal, cumulative, block_state = block_parts(*inputs_block)
    carried = apply_state(c_block, local_state, cumulative)
    new_state = jnp.exp(cumulative[-1])[..., None, None] * local_state + block_state
    return (
        (new_state, entry_total + cumulative[-1]),
        (diagonal + carried, cumulative + entry_total[None]),
    )


def entering_state(total, state, axis):
    count = lax.axis_size(axis)
    total, state = shifted((total, state), axis, 1)
    span = 1
    while span < count - 1:
        far_total, far_state = shifted((total, state), axis, span)
        state = jnp.exp(total)[..., None, None] * far_state + state
        total = total + far_total
        span *= 2
    return state


def body(
    inner_input,
    state_input,
    gate_input,
    step_logits,
    conv_inner,
    conv_states,
    bias_inner,
    bias_states,
    decay_log,
    skip_gain,
    norm_gain,
    out_weight,
):
    tokens = inner_input.shape[0]
    margin = CONV - 1
    previous = shifted((inner_input[tokens - margin :], state_input[tokens - margin :]), "ctx", 1)
    inner_conv = conv_silu(
        jnp.concatenate([previous[0], inner_input], axis=0), conv_inner, bias_inner, tokens
    )
    state_conv = conv_silu(
        jnp.concatenate([previous[1], state_input], axis=0), conv_states, bias_states, tokens
    )
    groups_here = state_input.shape[2] // STATE
    per_group = SSM_HEAD_COUNT // GROUPS
    blocks = tokens // BLK
    step_sizes = jax.nn.softplus(step_logits)
    log_rates = -step_sizes * jnp.exp(decay_log)[None]
    c_all = state_conv[:, 1].reshape(blocks, BLK, groups_here, STATE)
    inputs_all = (
        inner_conv.reshape(blocks, BLK, groups_here, per_group, HEAD_DIM),
        state_conv[:, 0].reshape(blocks, BLK, groups_here, STATE),
        c_all,
        step_sizes.reshape(blocks, BLK, groups_here, per_group),
        log_rates.reshape(blocks, BLK, groups_here, per_group),
    )
    if blocks == 1:
        diagonal, cumulative, local_state = block_parts(*(x[0] for x in inputs_all))
        partial_heads = diagonal[None]
        factors = cumulative[None]
        device_total = cumulative[-1]
    else:
        start_state = jnp.zeros((groups_here, per_group, HEAD_DIM, STATE), jnp.float32)
        start_total = jnp.zeros((groups_here, per_group), jnp.float32)
        (local_state, device_total), (partial_heads, factors) = lax.scan(
            block_local, (start_state, start_total), inputs_all
        )
    state_in = entering_state(device_total, local_state, "ctx")
    correction = jax.vmap(apply_state, in_axes=(0, None, 0))(c_all, state_in, factors)
    width_here = groups_here * per_group * HEAD_DIM
    mixed_heads = (partial_heads + correction).reshape(tokens, width_here) + jnp.repeat(
        skip_gain, HEAD_DIM
    )[None] * inner_conv.astype(jnp.float32)
    gated_out = mixed_heads * jax.nn.silu(gate_input.astype(jnp.float32))
    grouped = gated_out.reshape(tokens, groups_here, width_here // groups_here)
    normed = grouped * lax.rsqrt(jnp.mean(grouped * grouped, axis=-1, keepdims=True) + epsilon)
    normed = (normed.reshape(tokens, width_here) * norm_gain.astype(jnp.float32)).astype(
        jnp.bfloat16
    )
    return lax.psum_scatter(
        jnp.dot(normed, out_weight, preferred_element_type=jnp.float32).astype(jnp.bfloat16),
        "tp",
        scatter_dimension=0,
        tiled=True,
    )


def solution(mesh):
    placed = (
        P("ctx", "tp"),
        P("ctx", None, "tp"),
        P("ctx", "tp"),
        P("ctx", "tp"),
        P(None, "tp"),
        P(None, None, "tp"),
        P("tp"),
        P(None, "tp"),
        P("tp"),
        P("tp"),
        P("tp"),
        P("tp", None),
    )
    return jax.shard_map(
        body, mesh=mesh, in_specs=placed, out_specs=P(("ctx", "tp"), None), check_vma=False
    )
```

```python
import jax
import jax.numpy as jnp
from jax import lax
from jax.sharding import Mesh, PartitionSpec as P

SSM_HEAD_COUNT = 128
HEAD_DIM = 64
STATE = 128
GROUPS = 8
CONV = 4
BLK = 512


epsilon = 1e-05


def shifted(value, axis, by):
    count = lax.axis_size(axis)
    pairs = [(i, i + by) for i in range(count) if 0 <= i + by < count]
    return lax.ppermute(value, axis, pairs)


def conv_silu(padded, weight, offsets, row_count):
    summed = offsets.astype(jnp.float32)
    for k in range(CONV):
        summed = summed + weight[k].astype(jnp.float32) * padded[k : k + row_count].astype(
            jnp.float32
        )
    return lax.optimization_barrier(jax.nn.silu(summed).astype(jnp.bfloat16))


def block_parts(inner_block, b_block, c_block, step_sizes, log_rates):
    length = inner_block.shape[0]
    cumulative = jnp.cumsum(log_rates, axis=0)
    along = jnp.transpose(cumulative, (1, 2, 0))
    causal = lax.broadcasted_iota(jnp.int32, (length, length), 0) >= lax.broadcasted_iota(
        jnp.int32, (length, length), 1
    )
    decays = jnp.exp(jnp.where(causal, along[:, :, :, None] - along[:, :, None, :], -jnp.inf))
    scores = jnp.einsum("ign,jgn->gij", c_block, b_block, preferred_element_type=jnp.float32)
    mixing = (
        decays * scores[:, None] * jnp.transpose(step_sizes, (1, 2, 0))[:, :, None, :]
    ).astype(jnp.bfloat16)
    diagonal = jnp.einsum(
        "ghij,jghp->ighp", mixing, inner_block, preferred_element_type=jnp.float32
    )
    tail_weight = jnp.exp(cumulative[-1][None] - cumulative) * step_sizes
    weighted = (inner_block * tail_weight[..., None]).astype(jnp.bfloat16)
    block_state = jnp.einsum(
        "jghp,jgn->ghpn", weighted, b_block, preferred_element_type=jnp.float32
    )
    return diagonal, cumulative, block_state


def apply_state(c_block, state, cumulative):
    return jnp.exp(cumulative)[..., None] * jnp.einsum(
        "ign,ghpn->ighp", c_block.astype(jnp.float32), state, precision=lax.Precision.HIGHEST
    )


def block_local(carried_in, inputs_block):
    local_state, entry_total = carried_in
    inner_block, b_block, c_block, step_sizes, log_rates = inputs_block
    diagonal, cumulative, block_state = block_parts(*inputs_block)
    carried = apply_state(c_block, local_state, cumulative)
    new_state = jnp.exp(cumulative[-1])[..., None, None] * local_state + block_state
    return (
        (new_state, entry_total + cumulative[-1]),
        (diagonal + carried, cumulative + entry_total[None]),
    )


def pack(weight, state):
    rows = state.reshape(-1, state.shape[-1])
    high = weight.astype(jnp.bfloat16)
    low = (weight - high.astype(jnp.float32)).astype(jnp.bfloat16)
    lanes = rows.shape[-1]
    flat = jnp.concatenate([high.reshape(-1), low.reshape(-1)])
    pad = (-flat.shape[0]) % (16 * lanes)
    tail = jnp.pad(flat, (0, pad)).reshape(-1, lanes)
    return jnp.concatenate([rows.astype(jnp.bfloat16), tail], axis=0)


def unpack(packed, weight_shape, state_shape):
    count = 1
    for size in state_shape[:-1]:
        count *= size
    state = packed[:count].astype(jnp.float32).reshape(state_shape)
    flat = packed[count:].reshape(-1).astype(jnp.float32)
    size = 1
    for s in weight_shape:
        size *= s
    weight = (flat[:size] + flat[size : 2 * size]).reshape(weight_shape)
    return weight, state


def entering_state(total, state, axis):
    count = lax.axis_size(axis)
    weight = jnp.exp(total)
    if count == 1:
        return jnp.zeros_like(state)
    own = pack(weight, state)
    near_w, near_s = unpack(shifted(own, axis, 1), weight.shape, state.shape)
    if count == 2:
        return near_s
    far_w, far_s = unpack(shifted(own, axis, 2), weight.shape, state.shape)
    state = near_w[..., None, None] * far_s + near_s
    weight = near_w * far_w
    span = 2
    while 2 * span < count:
        far_w, far_s = unpack(shifted(pack(weight, state), axis, span), weight.shape, state.shape)
        state = weight[..., None, None] * far_s + state
        weight = weight * far_w
        span *= 2
    far = shifted(state.astype(jnp.bfloat16), axis, span).astype(jnp.float32)
    return weight[..., None, None] * far + state


def body(
    inner_input,
    state_input,
    gate_input,
    step_logits,
    conv_inner,
    conv_states,
    bias_inner,
    bias_states,
    decay_log,
    skip_gain,
    norm_gain,
    out_weight,
):
    tokens = inner_input.shape[0]
    margin = CONV - 1
    inner_width = inner_input.shape[1]
    halo = jnp.concatenate(
        [inner_input[tokens - margin :], state_input[tokens - margin :].reshape(margin, -1)], axis=1
    )
    halo = shifted(halo, "ctx", 1)
    inner_conv = conv_silu(
        jnp.concatenate([halo[:, :inner_width], inner_input], axis=0), conv_inner, bias_inner, tokens
    )
    state_conv = conv_silu(
        jnp.concatenate([halo[:, inner_width:].reshape((margin,) + state_input.shape[1:]), state_input], axis=0),
        conv_states,
        bias_states,
        tokens,
    )
    groups_here = state_input.shape[2] // STATE
    per_group = SSM_HEAD_COUNT // GROUPS
    blocks = tokens // BLK
    step_sizes = jax.nn.softplus(step_logits)
    log_rates = -step_sizes * jnp.exp(decay_log)[None]
    c_all = state_conv[:, 1].reshape(blocks, BLK, groups_here, STATE)
    inputs_all = (
        inner_conv.reshape(blocks, BLK, groups_here, per_group, HEAD_DIM),
        state_conv[:, 0].reshape(blocks, BLK, groups_here, STATE),
        c_all,
        step_sizes.reshape(blocks, BLK, groups_here, per_group),
        log_rates.reshape(blocks, BLK, groups_here, per_group),
    )
    if blocks == 1:
        diagonal, cumulative, local_state = block_parts(*(x[0] for x in inputs_all))
        partial_heads = diagonal[None]
        factors = cumulative[None]
        device_total = cumulative[-1]
    else:
        start_state = jnp.zeros((groups_here, per_group, HEAD_DIM, STATE), jnp.float32)
        start_total = jnp.zeros((groups_here, per_group), jnp.float32)
        (local_state, device_total), (partial_heads, factors) = lax.scan(
            block_local, (start_state, start_total), inputs_all
        )
    state_in = entering_state(device_total, local_state, "ctx")
    correction = jax.vmap(apply_state, in_axes=(0, None, 0))(c_all, state_in, factors)
    width_here = groups_here * per_group * HEAD_DIM
    mixed_heads = (partial_heads + correction).reshape(tokens, width_here) + jnp.repeat(
        skip_gain, HEAD_DIM
    )[None] * inner_conv.astype(jnp.float32)
    gated_out = mixed_heads * jax.nn.silu(gate_input.astype(jnp.float32))
    grouped = gated_out.reshape(tokens, groups_here, width_here // groups_here)
    normed = grouped * lax.rsqrt(jnp.mean(grouped * grouped, axis=-1, keepdims=True) + epsilon)
    normed = (normed.reshape(tokens, width_here) * norm_gain.astype(jnp.float32)).astype(
        jnp.bfloat16
    )
    projected = jnp.dot(normed, out_weight, preferred_element_type=jnp.float32).astype(jnp.bfloat16)
    outer = lax.axis_size("ty")
    inner = lax.axis_size("tc")
    piece = tokens // (outer * inner)
    projected = projected.reshape(outer, inner, piece, -1).transpose(1, 0, 2, 3)
    projected = lax.psum_scatter(projected, "tc", scatter_dimension=0, tiled=True)
    projected = lax.psum_scatter(projected[0], "ty", scatter_dimension=0, tiled=True)
    return projected.reshape(piece, -1)


def solution(mesh):
    cores = 2
    split = Mesh(
        mesh.devices.reshape(mesh.shape["ctx"], mesh.shape["tp"] // cores, cores),
        ("ctx", "ty", "tc"),
    )
    tp = ("ty", "tc")
    placed = (
        P("ctx", tp),
        P("ctx", None, tp),
        P("ctx", tp),
        P("ctx", tp),
        P(None, tp),
        P(None, None, tp),
        P(tp),
        P(None, tp),
        P(tp),
        P(tp),
        P(tp),
        P(tp, None),
    )
    return jax.shard_map(
        body, mesh=split, in_specs=placed, out_specs=P(("ctx",) + tp, None), check_vma=False
    )
```

```python
import jax
import jax.numpy as jnp
from jax import lax
from jax.sharding import Mesh, PartitionSpec as P

SSM_HEAD_COUNT = 128
HEAD_DIM = 64
STATE = 128
GROUPS = 8
CONV = 4
BLK = 512


epsilon = 1e-05


def shifted(value, axis, by):
    count = lax.axis_size(axis)
    pairs = [(i, i + by) for i in range(count) if 0 <= i + by < count]
    return lax.ppermute(value, axis, pairs)


def conv_silu(padded, weight, offsets, row_count):
    summed = offsets.astype(jnp.float32)
    for k in range(CONV):
        summed = summed + weight[k].astype(jnp.float32) * padded[k : k + row_count].astype(
            jnp.float32
        )
    return lax.optimization_barrier(jax.nn.silu(summed).astype(jnp.bfloat16))


def block_parts(inner_block, b_block, c_block, step_sizes, log_rates):
    length = inner_block.shape[0]
    cumulative = jnp.cumsum(log_rates, axis=0)
    along = jnp.transpose(cumulative, (1, 2, 0))
    causal = lax.broadcasted_iota(jnp.int32, (length, length), 0) >= lax.broadcasted_iota(
        jnp.int32, (length, length), 1
    )
    decays = jnp.exp(jnp.where(causal, along[:, :, :, None] - along[:, :, None, :], -jnp.inf))
    scores = jnp.einsum("ign,jgn->gij", c_block, b_block, preferred_element_type=jnp.float32)
    mixing = (
        decays * scores[:, None] * jnp.transpose(step_sizes, (1, 2, 0))[:, :, None, :]
    ).astype(jnp.bfloat16)
    diagonal = jnp.einsum(
        "ghij,jghp->ighp", mixing, inner_block, preferred_element_type=jnp.float32
    )
    tail_weight = jnp.exp(cumulative[-1][None] - cumulative) * step_sizes
    weighted = (inner_block * tail_weight[..., None]).astype(jnp.bfloat16)
    block_state = jnp.einsum(
        "jghp,jgn->ghpn", weighted, b_block, preferred_element_type=jnp.float32
    )
    return diagonal, cumulative, block_state


def apply_state(c_block, state, cumulative):
    return jnp.exp(cumulative)[..., None] * jnp.einsum(
        "ign,ghpn->ighp", c_block.astype(jnp.float32), state, precision=lax.Precision.HIGHEST
    )


def block_local(carried_in, inputs_block):
    local_state, entry_total = carried_in
    inner_block, b_block, c_block, step_sizes, log_rates = inputs_block
    diagonal, cumulative, block_state = block_parts(*inputs_block)
    carried = apply_state(c_block, local_state, cumulative)
    new_state = jnp.exp(cumulative[-1])[..., None, None] * local_state + block_state
    return (
        (new_state, entry_total + cumulative[-1]),
        (diagonal + carried, cumulative + entry_total[None]),
    )


def pack(weight, state):
    rows = state.reshape(-1, state.shape[-1])
    high = weight.astype(jnp.bfloat16)
    low = (weight - high.astype(jnp.float32)).astype(jnp.bfloat16)
    lanes = rows.shape[-1]
    flat = jnp.concatenate([high.reshape(-1), low.reshape(-1)])
    pad = (-flat.shape[0]) % (16 * lanes)
    tail = jnp.pad(flat, (0, pad)).reshape(-1, lanes)
    return jnp.concatenate([rows.astype(jnp.bfloat16), tail], axis=0)


def unpack(packed, weight_shape, state_shape):
    count = 1
    for size in state_shape[:-1]:
        count *= size
    state = packed[:count].astype(jnp.float32).reshape(state_shape)
    flat = packed[count:].reshape(-1).astype(jnp.float32)
    size = 1
    for s in weight_shape:
        size *= s
    weight = (flat[:size] + flat[size : 2 * size]).reshape(weight_shape)
    return weight, state


def entering_state(total, state, axis):
    count = lax.axis_size(axis)
    weight = jnp.exp(total)
    if count == 1:
        return jnp.zeros_like(state)
    own = pack(weight, state)
    near_w, near_s = unpack(shifted(own, axis, 1), weight.shape, state.shape)
    if count == 2:
        return near_s
    far_w, far_s = unpack(shifted(own, axis, 2), weight.shape, state.shape)
    state = near_w[..., None, None] * far_s + near_s
    weight = near_w * far_w
    span = 2
    while 2 * span < count:
        far_w, far_s = unpack(shifted(pack(weight, state), axis, span), weight.shape, state.shape)
        state = weight[..., None, None] * far_s + state
        weight = weight * far_w
        span *= 2
    far = shifted(state.astype(jnp.bfloat16), axis, span).astype(jnp.float32)
    return weight[..., None, None] * far + state


def body(
    inner_input,
    state_input,
    gate_input,
    step_logits,
    conv_inner,
    conv_states,
    bias_inner,
    bias_states,
    decay_log,
    skip_gain,
    norm_gain,
    out_weight,
):
    tokens = inner_input.shape[0]
    margin = CONV - 1
    inner_width = inner_input.shape[1]
    halo = jnp.concatenate(
        [inner_input[tokens - margin :], state_input[tokens - margin :].reshape(margin, -1)], axis=1
    )
    halo = shifted(halo, "ctx", 1)
    inner_conv = conv_silu(
        jnp.concatenate([halo[:, :inner_width], inner_input], axis=0), conv_inner, bias_inner, tokens
    )
    state_conv = conv_silu(
        jnp.concatenate([halo[:, inner_width:].reshape((margin,) + state_input.shape[1:]), state_input], axis=0),
        conv_states,
        bias_states,
        tokens,
    )
    groups_here = state_input.shape[2] // STATE
    per_group = SSM_HEAD_COUNT // GROUPS
    blocks = tokens // BLK
    step_sizes = jax.nn.softplus(step_logits)
    log_rates = -step_sizes * jnp.exp(decay_log)[None]
    c_all = state_conv[:, 1].reshape(blocks, BLK, groups_here, STATE)
    inputs_all = (
        inner_conv.reshape(blocks, BLK, groups_here, per_group, HEAD_DIM),
        state_conv[:, 0].reshape(blocks, BLK, groups_here, STATE),
        c_all,
        step_sizes.reshape(blocks, BLK, groups_here, per_group),
        log_rates.reshape(blocks, BLK, groups_here, per_group),
    )
    if blocks == 1:
        diagonal, cumulative, local_state = block_parts(*(x[0] for x in inputs_all))
        partial_heads = diagonal[None]
        factors = cumulative[None]
        device_total = cumulative[-1]
    else:
        start_state = jnp.zeros((groups_here, per_group, HEAD_DIM, STATE), jnp.float32)
        start_total = jnp.zeros((groups_here, per_group), jnp.float32)
        (local_state, device_total), (partial_heads, factors) = lax.scan(
            block_local, (start_state, start_total), inputs_all
        )
    state_in = entering_state(device_total, local_state, "ctx")
    correction = jax.vmap(apply_state, in_axes=(0, None, 0))(c_all, state_in, factors)
    width_here = groups_here * per_group * HEAD_DIM
    mixed_heads = (partial_heads + correction).reshape(tokens, width_here) + jnp.repeat(
        skip_gain, HEAD_DIM
    )[None] * inner_conv.astype(jnp.float32)
    gated_out = mixed_heads * jax.nn.silu(gate_input.astype(jnp.float32))
    grouped = gated_out.reshape(tokens, groups_here, width_here // groups_here)
    normed = grouped * lax.rsqrt(jnp.mean(grouped * grouped, axis=-1, keepdims=True) + epsilon)
    normed = (normed.reshape(tokens, width_here) * norm_gain.astype(jnp.float32)).astype(
        jnp.bfloat16
    )
    return reduce_rows(normed, out_weight)


def swap(value, axis):
    return lax.ppermute(value, axis, [(0, 1), (1, 0)])


def reduce_rows(normed, out_weight):
    tokens = normed.shape[0]
    outer = lax.axis_size("ty")
    inner = lax.axis_size("tc")
    piece = tokens // (outer * inner)
    ty = lax.axis_index("ty")
    tc = lax.axis_index("tc")
    rows = normed.reshape(outer, inner, piece, -1)

    def project(block):
        partial = jnp.dot(block, out_weight, preferred_element_type=jnp.float32)
        return partial.astype(jnp.bfloat16)

    def quarter(a, b):
        block = lax.dynamic_index_in_dim(rows, a, 0, keepdims=False)
        return lax.dynamic_index_in_dim(block, b, 0, keepdims=False)

    if inner != 2:
        projected = project(normed).reshape(outer, inner, piece, -1).reshape(outer * inner, piece, -1)
        return lax.psum_scatter(projected, ("ty", "tc"), scatter_dimension=0, tiled=True)[0]
    other = 1 - tc
    if outer == 2:
        far = 1 - ty
        sent_far = swap(project(quarter(far, other)), "tc")
        sent_near = swap(project(quarter(ty, other)), "tc")
        half = project(quarter(far, tc)).astype(jnp.float32) + sent_far.astype(jnp.float32)
        across = lax.ppermute(half.astype(jnp.bfloat16), "ty", [(0, 1), (1, 0)])
        mine = project(quarter(ty, tc)).astype(jnp.float32) + sent_near.astype(jnp.float32)
        return (mine + across.astype(jnp.float32)).astype(jnp.bfloat16)
    block = lax.dynamic_index_in_dim(rows, other, 1, keepdims=False)
    sent = swap(project(block.reshape(outer * piece, -1)), "tc")
    block = lax.dynamic_index_in_dim(rows, tc, 1, keepdims=False)
    half = project(block.reshape(outer * piece, -1)).astype(jnp.float32) + sent.astype(jnp.float32)
    half = half.astype(jnp.bfloat16).reshape(outer, piece, -1)
    return lax.psum_scatter(half, "ty", scatter_dimension=0, tiled=True)[0]


def solution(mesh):
    cores = 2
    split = Mesh(
        mesh.devices.reshape(mesh.shape["ctx"], mesh.shape["tp"] // cores, cores),
        ("ctx", "ty", "tc"),
    )
    tp = ("ty", "tc")
    placed = (
        P("ctx", tp),
        P("ctx", None, tp),
        P("ctx", tp),
        P("ctx", tp),
        P(None, tp),
        P(None, None, tp),
        P(tp),
        P(None, tp),
        P(tp),
        P(tp),
        P(tp),
        P(tp, None),
    )
    return jax.shard_map(
        body, mesh=split, in_specs=placed, out_specs=P(("ctx",) + tp, None), check_vma=False
    )
```

```python
import jax
import jax.numpy as jnp
from jax import lax
from jax.sharding import Mesh, PartitionSpec as P

SSM_HEAD_COUNT = 128
HEAD_DIM = 64
STATE = 128
GROUPS = 8
CONV = 4
BLK = 512


epsilon = 1e-05


def shifted(value, axis, by):
    count = lax.axis_size(axis)
    pairs = [(i, i + by) for i in range(count) if 0 <= i + by < count]
    return lax.ppermute(value, axis, pairs)


def conv_silu(padded, weight, offsets, row_count):
    summed = offsets.astype(jnp.float32)
    for k in range(CONV):
        summed = summed + weight[k].astype(jnp.float32) * padded[k : k + row_count].astype(
            jnp.float32
        )
    return lax.optimization_barrier(jax.nn.silu(summed).astype(jnp.bfloat16))


def block_parts(inner_block, b_block, c_block, step_sizes, log_rates):
    length = inner_block.shape[0]
    cumulative = jnp.cumsum(log_rates, axis=0)
    along = jnp.transpose(cumulative, (1, 2, 0))
    causal = lax.broadcasted_iota(jnp.int32, (length, length), 0) >= lax.broadcasted_iota(
        jnp.int32, (length, length), 1
    )
    decays = jnp.exp(jnp.where(causal, along[:, :, :, None] - along[:, :, None, :], -jnp.inf))
    scores = jnp.einsum("ign,jgn->gij", c_block, b_block, preferred_element_type=jnp.float32)
    mixing = (
        decays * scores[:, None] * jnp.transpose(step_sizes, (1, 2, 0))[:, :, None, :]
    ).astype(jnp.bfloat16)
    diagonal = jnp.einsum(
        "ghij,jghp->ighp", mixing, inner_block, preferred_element_type=jnp.float32
    )
    tail_weight = jnp.exp(cumulative[-1][None] - cumulative) * step_sizes
    weighted = (inner_block * tail_weight[..., None]).astype(jnp.bfloat16)
    block_state = jnp.einsum(
        "jghp,jgn->ghpn", weighted, b_block, preferred_element_type=jnp.float32
    )
    return diagonal, cumulative, block_state


def apply_state(c_block, state, cumulative):
    return jnp.exp(cumulative)[..., None] * jnp.einsum(
        "ign,ghpn->ighp", c_block.astype(jnp.float32), state, precision=lax.Precision.HIGHEST
    )


def block_local(carried_in, inputs_block):
    local_state, entry_total = carried_in
    inner_block, b_block, c_block, step_sizes, log_rates = inputs_block
    diagonal, cumulative, block_state = block_parts(*inputs_block)
    carried = apply_state(c_block, local_state, cumulative)
    new_state = jnp.exp(cumulative[-1])[..., None, None] * local_state + block_state
    return (
        (new_state, entry_total + cumulative[-1]),
        (diagonal + carried, cumulative + entry_total[None]),
    )


def pack(weight, state):
    rows = state.reshape(-1, state.shape[-1])
    high = weight.astype(jnp.bfloat16)
    low = (weight - high.astype(jnp.float32)).astype(jnp.bfloat16)
    lanes = rows.shape[-1]
    flat = jnp.concatenate([high.reshape(-1), low.reshape(-1)])
    pad = (-flat.shape[0]) % (16 * lanes)
    tail = jnp.pad(flat, (0, pad)).reshape(-1, lanes)
    return jnp.concatenate([rows.astype(jnp.bfloat16), tail], axis=0)


def unpack(packed, weight_shape, state_shape):
    count = 1
    for size in state_shape[:-1]:
        count *= size
    state = packed[:count].astype(jnp.float32).reshape(state_shape)
    flat = packed[count:].reshape(-1).astype(jnp.float32)
    size = 1
    for s in weight_shape:
        size *= s
    weight = (flat[:size] + flat[size : 2 * size]).reshape(weight_shape)
    return weight, state


def entering_state(total, state, axis):
    count = lax.axis_size(axis)
    weight = jnp.exp(total)
    if count == 1:
        return jnp.zeros_like(state)
    own = pack(weight, state)
    near_w, near_s = unpack(shifted(own, axis, 1), weight.shape, state.shape)
    if count == 2:
        return near_s
    far_w, far_s = unpack(shifted(own, axis, 2), weight.shape, state.shape)
    state = near_w[..., None, None] * far_s + near_s
    weight = near_w * far_w
    span = 2
    while 2 * span < count:
        far_w, far_s = unpack(shifted(pack(weight, state), axis, span), weight.shape, state.shape)
        state = weight[..., None, None] * far_s + state
        weight = weight * far_w
        span *= 2
    far = shifted(state.astype(jnp.bfloat16), axis, span).astype(jnp.float32)
    return weight[..., None, None] * far + state


def body(
    inner_input,
    state_input,
    gate_input,
    step_logits,
    conv_inner,
    conv_states,
    bias_inner,
    bias_states,
    decay_log,
    skip_gain,
    norm_gain,
    out_weight,
):
    tokens = inner_input.shape[0]
    margin = CONV - 1
    inner_width = inner_input.shape[1]
    halo = jnp.concatenate(
        [inner_input[tokens - margin :], state_input[tokens - margin :].reshape(margin, -1)], axis=1
    )
    halo = shifted(halo, "ctx", 1)
    inner_conv = conv_silu(
        jnp.concatenate([halo[:, :inner_width], inner_input], axis=0), conv_inner, bias_inner, tokens
    )
    state_conv = conv_silu(
        jnp.concatenate([halo[:, inner_width:].reshape((margin,) + state_input.shape[1:]), state_input], axis=0),
        conv_states,
        bias_states,
        tokens,
    )
    groups_here = state_input.shape[2] // STATE
    per_group = SSM_HEAD_COUNT // GROUPS
    blocks = tokens // BLK
    step_sizes = jax.nn.softplus(step_logits)
    log_rates = -step_sizes * jnp.exp(decay_log)[None]
    c_all = state_conv[:, 1].reshape(blocks, BLK, groups_here, STATE)
    inputs_all = (
        inner_conv.reshape(blocks, BLK, groups_here, per_group, HEAD_DIM),
        state_conv[:, 0].reshape(blocks, BLK, groups_here, STATE),
        c_all,
        step_sizes.reshape(blocks, BLK, groups_here, per_group),
        log_rates.reshape(blocks, BLK, groups_here, per_group),
    )
    if blocks == 1:
        diagonal, cumulative, local_state = block_parts(*(x[0] for x in inputs_all))
        partial_heads = diagonal[None]
        factors = cumulative[None]
        device_total = cumulative[-1]
    else:
        start_state = jnp.zeros((groups_here, per_group, HEAD_DIM, STATE), jnp.float32)
        start_total = jnp.zeros((groups_here, per_group), jnp.float32)
        (local_state, device_total), (partial_heads, factors) = lax.scan(
            block_local, (start_state, start_total), inputs_all
        )
    state_in = entering_state(device_total, local_state, "ctx")
    correction = jax.vmap(apply_state, in_axes=(0, None, 0))(c_all, state_in, factors)
    width_here = groups_here * per_group * HEAD_DIM
    mixed_heads = (partial_heads + correction).reshape(tokens, width_here) + jnp.repeat(
        skip_gain, HEAD_DIM
    )[None] * inner_conv.astype(jnp.float32)
    gated_out = mixed_heads * jax.nn.silu(gate_input.astype(jnp.float32))
    grouped = gated_out.reshape(tokens, groups_here, width_here // groups_here)
    normed = grouped * lax.rsqrt(jnp.mean(grouped * grouped, axis=-1, keepdims=True) + epsilon)
    normed = (normed.reshape(tokens, width_here) * norm_gain.astype(jnp.float32)).astype(
        jnp.bfloat16
    )
    return reduce_rows(normed, out_weight)


def swap(value, axis):
    return lax.ppermute(value, axis, [(0, 1), (1, 0)])


def reduce_rows(normed, out_weight):
    tokens = normed.shape[0]
    outer = lax.axis_size("ty")
    inner = lax.axis_size("tc")
    piece = tokens // (outer * inner)
    ty = lax.axis_index("ty")
    tc = lax.axis_index("tc")

    def project(block):
        partial = jnp.dot(block, out_weight, preferred_element_type=jnp.float32)
        return partial.astype(jnp.bfloat16)

    if inner != 2:
        projected = project(normed).reshape(outer * inner, piece, -1)
        return lax.psum_scatter(projected, ("ty", "tc"), scatter_dimension=0, tiled=True)[0]
    other = 1 - tc
    width = out_weight.shape[1]
    chunks = 4 if width % (4 * 128) == 0 else 1
    step = width // chunks
    done = []
    for c in range(chunks):
        partial = jnp.dot(
            normed, out_weight[:, c * step : (c + 1) * step], preferred_element_type=jnp.float32
        ).astype(jnp.bfloat16)
        partial = partial.reshape(outer, inner, piece, step)
        sent = swap(lax.dynamic_index_in_dim(partial, other, 1, keepdims=False), "tc")
        half = lax.dynamic_index_in_dim(partial, tc, 1, keepdims=False).astype(jnp.float32)
        half = half + sent.astype(jnp.float32)
        if outer == 2:
            across = swap(
                lax.dynamic_index_in_dim(half, 1 - ty, 0, keepdims=False).astype(jnp.bfloat16), "ty"
            )
            mine = lax.dynamic_index_in_dim(half, ty, 0, keepdims=False)
            done.append((mine + across.astype(jnp.float32)).astype(jnp.bfloat16))
        else:
            done.append(
                lax.psum_scatter(half.astype(jnp.bfloat16), "ty", scatter_dimension=0, tiled=True)[0]
            )
    return jnp.concatenate(done, axis=1)


def solution(mesh):
    cores = 2
    split = Mesh(
        mesh.devices.reshape(mesh.shape["ctx"], mesh.shape["tp"] // cores, cores),
        ("ctx", "ty", "tc"),
    )
    tp = ("ty", "tc")
    placed = (
        P("ctx", tp),
        P("ctx", None, tp),
        P("ctx", tp),
        P("ctx", tp),
        P(None, tp),
        P(None, None, tp),
        P(tp),
        P(None, tp),
        P(tp),
        P(tp),
        P(tp),
        P(tp, None),
    )
    return jax.shard_map(
        body, mesh=split, in_specs=placed, out_specs=P(("ctx",) + tp, None), check_vma=False
    )
```

```python
import jax
import jax.numpy as jnp
from jax import lax
from jax.sharding import Mesh, PartitionSpec as P

SSM_HEAD_COUNT = 128
HEAD_DIM = 64
STATE = 128
GROUPS = 8
CONV = 4
BLK = 512


epsilon = 1e-05


def shifted(value, axis, by):
    count = lax.axis_size(axis)
    pairs = [(i, i + by) for i in range(count) if 0 <= i + by < count]
    return lax.ppermute(value, axis, pairs)


def conv_silu(padded, weight, offsets, row_count):
    summed = offsets.astype(jnp.float32)
    for k in range(CONV):
        summed = summed + weight[k].astype(jnp.float32) * padded[k : k + row_count].astype(
            jnp.float32
        )
    return lax.optimization_barrier(jax.nn.silu(summed).astype(jnp.bfloat16))


def block_parts(inner_block, b_block, c_block, step_sizes, log_rates):
    length = inner_block.shape[0]
    cumulative = jnp.cumsum(log_rates, axis=0)
    along = jnp.transpose(cumulative, (1, 2, 0))
    causal = lax.broadcasted_iota(jnp.int32, (length, length), 0) >= lax.broadcasted_iota(
        jnp.int32, (length, length), 1
    )
    decays = jnp.exp(jnp.where(causal, along[:, :, :, None] - along[:, :, None, :], -jnp.inf))
    scores = jnp.einsum("ign,jgn->gij", c_block, b_block, preferred_element_type=jnp.float32)
    mixing = (
        decays * scores[:, None] * jnp.transpose(step_sizes, (1, 2, 0))[:, :, None, :]
    ).astype(jnp.bfloat16)
    diagonal = jnp.einsum(
        "ghij,jghp->ighp", mixing, inner_block, preferred_element_type=jnp.float32
    )
    tail_weight = jnp.exp(cumulative[-1][None] - cumulative) * step_sizes
    weighted = (inner_block * tail_weight[..., None]).astype(jnp.bfloat16)
    block_state = jnp.einsum(
        "jghp,jgn->ghpn", weighted, b_block, preferred_element_type=jnp.float32
    )
    return diagonal, cumulative, block_state


def apply_state(c_block, state, cumulative):
    return jnp.exp(cumulative)[..., None] * jnp.einsum(
        "ign,ghpn->ighp", c_block.astype(jnp.float32), state, precision=lax.Precision.HIGHEST
    )


def block_local(carried_in, inputs_block):
    local_state, entry_total = carried_in
    inner_block, b_block, c_block, step_sizes, log_rates = inputs_block
    diagonal, cumulative, block_state = block_parts(*inputs_block)
    carried = apply_state(c_block, local_state, cumulative)
    new_state = jnp.exp(cumulative[-1])[..., None, None] * local_state + block_state
    return (
        (new_state, entry_total + cumulative[-1]),
        (diagonal + carried, cumulative + entry_total[None]),
    )


def pack(weight, state):
    rows = state.reshape(-1, state.shape[-1])
    high = weight.astype(jnp.bfloat16)
    low = (weight - high.astype(jnp.float32)).astype(jnp.bfloat16)
    lanes = rows.shape[-1]
    flat = jnp.concatenate([high.reshape(-1), low.reshape(-1)])
    pad = (-flat.shape[0]) % (16 * lanes)
    tail = jnp.pad(flat, (0, pad)).reshape(-1, lanes)
    return jnp.concatenate([rows.astype(jnp.bfloat16), tail], axis=0)


def unpack(packed, weight_shape, state_shape):
    count = 1
    for size in state_shape[:-1]:
        count *= size
    state = packed[:count].astype(jnp.float32).reshape(state_shape)
    flat = packed[count:].reshape(-1).astype(jnp.float32)
    size = 1
    for s in weight_shape:
        size *= s
    weight = (flat[:size] + flat[size : 2 * size]).reshape(weight_shape)
    return weight, state


def entering_state(total, state, axis):
    count = lax.axis_size(axis)
    weight = jnp.exp(total)
    if count == 1:
        return jnp.zeros_like(state)
    own = pack(weight, state)
    near_w, near_s = unpack(shifted(own, axis, 1), weight.shape, state.shape)
    if count == 2:
        return near_s
    far_w, far_s = unpack(shifted(own, axis, 2), weight.shape, state.shape)
    state = near_w[..., None, None] * far_s + near_s
    weight = near_w * far_w
    span = 2
    while 2 * span < count:
        far_w, far_s = unpack(shifted(pack(weight, state), axis, span), weight.shape, state.shape)
        state = weight[..., None, None] * far_s + state
        weight = weight * far_w
        span *= 2
    far = shifted(state.astype(jnp.bfloat16), axis, span).astype(jnp.float32)
    return weight[..., None, None] * far + state


def body(
    inner_input,
    state_input,
    gate_input,
    step_logits,
    conv_inner,
    conv_states,
    bias_inner,
    bias_states,
    decay_log,
    skip_gain,
    norm_gain,
    out_weight,
):
    tokens = inner_input.shape[0]
    margin = CONV - 1
    inner_width = inner_input.shape[1]
    halo = jnp.concatenate(
        [inner_input[tokens - margin :], state_input[tokens - margin :].reshape(margin, -1)], axis=1
    )
    halo = shifted(halo, "ctx", 1)
    inner_conv = conv_silu(
        jnp.concatenate([halo[:, :inner_width], inner_input], axis=0), conv_inner, bias_inner, tokens
    )
    state_conv = conv_silu(
        jnp.concatenate([halo[:, inner_width:].reshape((margin,) + state_input.shape[1:]), state_input], axis=0),
        conv_states,
        bias_states,
        tokens,
    )
    groups_here = state_input.shape[2] // STATE
    per_group = SSM_HEAD_COUNT // GROUPS
    blocks = tokens // BLK
    step_sizes = jax.nn.softplus(step_logits)
    log_rates = -step_sizes * jnp.exp(decay_log)[None]
    c_all = state_conv[:, 1].reshape(blocks, BLK, groups_here, STATE)
    inputs_all = (
        inner_conv.reshape(blocks, BLK, groups_here, per_group, HEAD_DIM),
        state_conv[:, 0].reshape(blocks, BLK, groups_here, STATE),
        c_all,
        step_sizes.reshape(blocks, BLK, groups_here, per_group),
        log_rates.reshape(blocks, BLK, groups_here, per_group),
    )
    if blocks == 1:
        diagonal, cumulative, local_state = block_parts(*(x[0] for x in inputs_all))
        partial_heads = diagonal[None]
        factors = cumulative[None]
        device_total = cumulative[-1]
    else:
        start_state = jnp.zeros((groups_here, per_group, HEAD_DIM, STATE), jnp.float32)
        start_total = jnp.zeros((groups_here, per_group), jnp.float32)
        (local_state, device_total), (partial_heads, factors) = lax.scan(
            block_local, (start_state, start_total), inputs_all
        )
    state_in = entering_state(device_total, local_state, "ctx")
    correction = jax.vmap(apply_state, in_axes=(0, None, 0))(c_all, state_in, factors)
    width_here = groups_here * per_group * HEAD_DIM
    mixed_heads = (partial_heads + correction).reshape(tokens, width_here) + jnp.repeat(
        skip_gain, HEAD_DIM
    )[None] * inner_conv.astype(jnp.float32)
    gated_out = mixed_heads * jax.nn.silu(gate_input.astype(jnp.float32))
    grouped = gated_out.reshape(tokens, groups_here, width_here // groups_here)
    normed = grouped * lax.rsqrt(jnp.mean(grouped * grouped, axis=-1, keepdims=True) + epsilon)
    normed = (normed.reshape(tokens, width_here) * norm_gain.astype(jnp.float32)).astype(
        jnp.bfloat16
    )
    return reduce_rows(normed, out_weight)


def swap(value, axis):
    return lax.ppermute(value, axis, [(0, 1), (1, 0)])


def reduce_rows(normed, out_weight):
    tokens = normed.shape[0]
    outer = lax.axis_size("ty")
    inner = lax.axis_size("tc")
    piece = tokens // (outer * inner)
    ty = lax.axis_index("ty")
    tc = lax.axis_index("tc")

    def project(block):
        partial = jnp.dot(block, out_weight, preferred_element_type=jnp.float32)
        return partial.astype(jnp.bfloat16)

    if inner != 2:
        projected = project(normed).reshape(outer * inner, piece, -1)
        return lax.psum_scatter(projected, ("ty", "tc"), scatter_dimension=0, tiled=True)[0]
    other = 1 - tc
    width = out_weight.shape[1]
    chunks = 4 if width % (4 * 128) == 0 else 1
    step = width // chunks
    done = []
    payloads = []
    for c in range(chunks):
        source = normed
        if c >= 2 and payloads[c - 2] is not None:
            payloads[c - 2], source = lax.optimization_barrier((payloads[c - 2], normed))
        partial = jnp.dot(
            source, out_weight[:, c * step : (c + 1) * step], preferred_element_type=jnp.float32
        ).astype(jnp.bfloat16)
        partial = partial.reshape(outer, inner, piece, step)
        sent = swap(lax.dynamic_index_in_dim(partial, other, 1, keepdims=False), "tc")
        half = lax.dynamic_index_in_dim(partial, tc, 1, keepdims=False).astype(jnp.float32)
        half = half + sent.astype(jnp.float32)
        if outer == 2:
            payloads.append(
                lax.dynamic_index_in_dim(half, 1 - ty, 0, keepdims=False).astype(jnp.bfloat16)
            )
        else:
            payloads.append(None)
        done.append(half)
    for c in range(chunks):
        half = done[c]
        if outer == 2:
            across = swap(payloads[c], "ty")
            mine = lax.dynamic_index_in_dim(half, ty, 0, keepdims=False)
            done[c] = (mine + across.astype(jnp.float32)).astype(jnp.bfloat16)
        else:
            done[c] = lax.psum_scatter(
                half.astype(jnp.bfloat16), "ty", scatter_dimension=0, tiled=True
            )[0]
    return jnp.concatenate(done, axis=1)


def solution(mesh):
    cores = 2
    split = Mesh(
        mesh.devices.reshape(mesh.shape["ctx"], mesh.shape["tp"] // cores, cores),
        ("ctx", "ty", "tc"),
    )
    tp = ("ty", "tc")
    placed = (
        P("ctx", tp),
        P("ctx", None, tp),
        P("ctx", tp),
        P("ctx", tp),
        P(None, tp),
        P(None, None, tp),
        P(tp),
        P(None, tp),
        P(tp),
        P(tp),
        P(tp),
        P(tp, None),
    )
    return jax.shard_map(
        body, mesh=split, in_specs=placed, out_specs=P(("ctx",) + tp, None), check_vma=False
    )
```

```python
import jax
import jax.numpy as jnp
from jax import lax
from jax.sharding import Mesh, PartitionSpec as P

SSM_HEAD_COUNT = 128
HEAD_DIM = 64
STATE = 128
GROUPS = 8
CONV = 4
BLK = 512


epsilon = 1e-05


def shifted(value, axis, by):
    count = lax.axis_size(axis)
    pairs = [(i, i + by) for i in range(count) if 0 <= i + by < count]
    return lax.ppermute(value, axis, pairs)


def conv_silu(padded, weight, offsets, row_count):
    summed = offsets.astype(jnp.float32)
    for k in range(CONV):
        summed = summed + weight[k].astype(jnp.float32) * padded[k : k + row_count].astype(
            jnp.float32
        )
    return lax.optimization_barrier(jax.nn.silu(summed).astype(jnp.bfloat16))


def block_parts(inner_block, b_block, c_block, step_sizes, log_rates):
    length = inner_block.shape[0]
    cumulative = jnp.cumsum(log_rates, axis=0)
    along = jnp.transpose(cumulative, (1, 2, 0))
    causal = lax.broadcasted_iota(jnp.int32, (length, length), 0) >= lax.broadcasted_iota(
        jnp.int32, (length, length), 1
    )
    decays = jnp.exp(jnp.where(causal, along[:, :, :, None] - along[:, :, None, :], -jnp.inf))
    scores = jnp.einsum("ign,jgn->gij", c_block, b_block, preferred_element_type=jnp.float32)
    mixing = (
        decays * scores[:, None] * jnp.transpose(step_sizes, (1, 2, 0))[:, :, None, :]
    ).astype(jnp.bfloat16)
    diagonal = jnp.einsum(
        "ghij,jghp->ighp", mixing, inner_block, preferred_element_type=jnp.float32
    )
    tail_weight = jnp.exp(cumulative[-1][None] - cumulative) * step_sizes
    weighted = (inner_block * tail_weight[..., None]).astype(jnp.bfloat16)
    block_state = jnp.einsum(
        "jghp,jgn->ghpn", weighted, b_block, preferred_element_type=jnp.float32
    )
    return diagonal, cumulative, block_state


def apply_state(c_block, state, cumulative):
    high = state.astype(jnp.bfloat16)
    rest = state - high.astype(jnp.float32)
    middle = rest.astype(jnp.bfloat16)
    low = (rest - middle.astype(jnp.float32)).astype(jnp.bfloat16)
    applied = sum(
        jnp.einsum("ign,ghpn->ighp", c_block, part, preferred_element_type=jnp.float32)
        for part in (low, middle, high)
    )
    return jnp.exp(cumulative)[..., None] * applied


def block_local(carried_in, inputs_block):
    local_state, entry_total = carried_in
    inner_block, b_block, c_block, step_sizes, log_rates = inputs_block
    diagonal, cumulative, block_state = block_parts(*inputs_block)
    carried = apply_state(c_block, local_state, cumulative)
    new_state = jnp.exp(cumulative[-1])[..., None, None] * local_state + block_state
    return (
        (new_state, entry_total + cumulative[-1]),
        (diagonal + carried, cumulative + entry_total[None]),
    )


def pack(weight, state):
    rows = state.reshape(-1, state.shape[-1])
    high = weight.astype(jnp.bfloat16)
    low = (weight - high.astype(jnp.float32)).astype(jnp.bfloat16)
    lanes = rows.shape[-1]
    flat = jnp.concatenate([high.reshape(-1), low.reshape(-1)])
    pad = (-flat.shape[0]) % (16 * lanes)
    tail = jnp.pad(flat, (0, pad)).reshape(-1, lanes)
    return jnp.concatenate([rows.astype(jnp.bfloat16), tail], axis=0)


def unpack(packed, weight_shape, state_shape):
    count = 1
    for size in state_shape[:-1]:
        count *= size
    state = packed[:count].astype(jnp.float32).reshape(state_shape)
    flat = packed[count:].reshape(-1).astype(jnp.float32)
    size = 1
    for s in weight_shape:
        size *= s
    weight = (flat[:size] + flat[size : 2 * size]).reshape(weight_shape)
    return weight, state


def entering_state(total, state, axis):
    count = lax.axis_size(axis)
    weight = jnp.exp(total)
    if count == 1:
        return jnp.zeros_like(state)
    own = pack(weight, state)
    near_w, near_s = unpack(shifted(own, axis, 1), weight.shape, state.shape)
    if count == 2:
        return near_s
    far_w, far_s = unpack(shifted(own, axis, 2), weight.shape, state.shape)
    state = near_w[..., None, None] * far_s + near_s
    weight = near_w * far_w
    span = 2
    while 2 * span < count:
        far_w, far_s = unpack(shifted(pack(weight, state), axis, span), weight.shape, state.shape)
        state = weight[..., None, None] * far_s + state
        weight = weight * far_w
        span *= 2
    far = shifted(state.astype(jnp.bfloat16), axis, span).astype(jnp.float32)
    return weight[..., None, None] * far + state


def body(
    inner_input,
    state_input,
    gate_input,
    step_logits,
    conv_inner,
    conv_states,
    bias_inner,
    bias_states,
    decay_log,
    skip_gain,
    norm_gain,
    out_weight,
):
    tokens = inner_input.shape[0]
    margin = CONV - 1
    inner_width = inner_input.shape[1]
    halo = jnp.concatenate(
        [inner_input[tokens - margin :], state_input[tokens - margin :].reshape(margin, -1)], axis=1
    )
    halo = shifted(halo, "ctx", 1)
    inner_conv = conv_silu(
        jnp.concatenate([halo[:, :inner_width], inner_input], axis=0), conv_inner, bias_inner, tokens
    )
    state_conv = conv_silu(
        jnp.concatenate([halo[:, inner_width:].reshape((margin,) + state_input.shape[1:]), state_input], axis=0),
        conv_states,
        bias_states,
        tokens,
    )
    groups_here = state_input.shape[2] // STATE
    per_group = SSM_HEAD_COUNT // GROUPS
    blocks = tokens // BLK
    step_sizes = jax.nn.softplus(step_logits)
    log_rates = -step_sizes * jnp.exp(decay_log)[None]
    c_all = state_conv[:, 1].reshape(blocks, BLK, groups_here, STATE)
    inputs_all = (
        inner_conv.reshape(blocks, BLK, groups_here, per_group, HEAD_DIM),
        state_conv[:, 0].reshape(blocks, BLK, groups_here, STATE),
        c_all,
        step_sizes.reshape(blocks, BLK, groups_here, per_group),
        log_rates.reshape(blocks, BLK, groups_here, per_group),
    )
    if blocks == 1:
        diagonal, cumulative, local_state = block_parts(*(x[0] for x in inputs_all))
        partial_heads = diagonal[None]
        factors = cumulative[None]
        device_total = cumulative[-1]
    else:
        start_state = jnp.zeros((groups_here, per_group, HEAD_DIM, STATE), jnp.float32)
        start_total = jnp.zeros((groups_here, per_group), jnp.float32)
        (local_state, device_total), (partial_heads, factors) = lax.scan(
            block_local, (start_state, start_total), inputs_all
        )
    state_in = entering_state(device_total, local_state, "ctx")
    correction = jax.vmap(apply_state, in_axes=(0, None, 0))(c_all, state_in, factors)
    width_here = groups_here * per_group * HEAD_DIM
    mixed_heads = (partial_heads + correction).reshape(tokens, width_here) + jnp.repeat(
        skip_gain, HEAD_DIM
    )[None] * inner_conv.astype(jnp.float32)
    gated_out = mixed_heads * jax.nn.silu(gate_input.astype(jnp.float32))
    grouped = gated_out.reshape(tokens, groups_here, width_here // groups_here)
    normed = grouped * lax.rsqrt(jnp.mean(grouped * grouped, axis=-1, keepdims=True) + epsilon)
    normed = (normed.reshape(tokens, width_here) * norm_gain.astype(jnp.float32)).astype(
        jnp.bfloat16
    )
    return reduce_rows(normed, out_weight)


def swap(value, axis):
    return lax.ppermute(value, axis, [(0, 1), (1, 0)])


def reduce_rows(normed, out_weight):
    tokens = normed.shape[0]
    outer = lax.axis_size("ty")
    inner = lax.axis_size("tc")
    piece = tokens // (outer * inner)
    ty = lax.axis_index("ty")
    tc = lax.axis_index("tc")

    def project(block):
        partial = jnp.dot(block, out_weight, preferred_element_type=jnp.float32)
        return partial.astype(jnp.bfloat16)

    if inner != 2:
        projected = project(normed).reshape(outer * inner, piece, -1)
        return lax.psum_scatter(projected, ("ty", "tc"), scatter_dimension=0, tiled=True)[0]
    other = 1 - tc
    width = out_weight.shape[1]
    chunks = 4 if width % (4 * 128) == 0 else 1
    step = width // chunks
    done = []
    for c in range(chunks):
        partial = jnp.dot(
            normed, out_weight[:, c * step : (c + 1) * step], preferred_element_type=jnp.float32
        ).astype(jnp.bfloat16)
        partial = partial.reshape(outer, inner, piece, step)
        sent = swap(lax.dynamic_index_in_dim(partial, other, 1, keepdims=False), "tc")
        half = lax.dynamic_index_in_dim(partial, tc, 1, keepdims=False).astype(jnp.float32)
        half = half + sent.astype(jnp.float32)
        if outer == 2:
            across = swap(
                lax.dynamic_index_in_dim(half, 1 - ty, 0, keepdims=False).astype(jnp.bfloat16), "ty"
            )
            mine = lax.dynamic_index_in_dim(half, ty, 0, keepdims=False)
            done.append((mine + across.astype(jnp.float32)).astype(jnp.bfloat16))
        else:
            done.append(
                lax.psum_scatter(half.astype(jnp.bfloat16), "ty", scatter_dimension=0, tiled=True)[0]
            )
    return jnp.concatenate(done, axis=1)


def solution(mesh):
    cores = 2
    split = Mesh(
        mesh.devices.reshape(mesh.shape["ctx"], mesh.shape["tp"] // cores, cores),
        ("ctx", "ty", "tc"),
    )
    tp = ("ty", "tc")
    placed = (
        P("ctx", tp),
        P("ctx", None, tp),
        P("ctx", tp),
        P("ctx", tp),
        P(None, tp),
        P(None, None, tp),
        P(tp),
        P(None, tp),
        P(tp),
        P(tp),
        P(tp),
        P(tp, None),
    )
    return jax.shard_map(
        body, mesh=split, in_specs=placed, out_specs=P(("ctx",) + tp, None), check_vma=False
    )
```

```python
import jax
import jax.numpy as jnp
from jax import lax
from jax.experimental import pallas as pl
from jax.experimental.pallas import tpu as pltpu
from jax.sharding import Mesh, PartitionSpec as P

SSM_HEAD_COUNT = 128
HEAD_DIM = 64
STATE = 128
GROUPS = 8
CONV = 4
BLK = 512


epsilon = 1e-05


def shifted(value, axis, by):
    count = lax.axis_size(axis)
    pairs = [(i, i + by) for i in range(count) if 0 <= i + by < count]
    return lax.ppermute(value, axis, pairs)


def conv_silu(padded, weight, offsets, row_count):
    summed = offsets.astype(jnp.float32)
    for k in range(CONV):
        summed = summed + weight[k].astype(jnp.float32) * padded[k : k + row_count].astype(
            jnp.float32
        )
    return lax.optimization_barrier(jax.nn.silu(summed).astype(jnp.bfloat16))


def conv_kernel(halo_ref, x_ref, w_ref, b_ref, o_ref, pad_ref):
    rows = x_ref.shape[0]
    pad_ref[0:8, :] = halo_ref[...].astype(jnp.float32)
    pad_ref[8 : 8 + rows, :] = x_ref[...].astype(jnp.float32)
    summed = b_ref[...].astype(jnp.float32)
    for k in range(CONV):
        summed = summed + w_ref[k : k + 1, :].astype(jnp.float32) * pad_ref[8 - (CONV - 1) + k : 8 - (CONV - 1) + k + rows, :]
    o_ref[...] = jax.nn.silu(summed).astype(o_ref.dtype)

def conv_silu_kernel(halo, x, weight, bias):
    rows, width = x.shape
    block = 512 if width % 512 == 0 else width
    halo8 = jnp.concatenate([jnp.zeros((8 - halo.shape[0], width), halo.dtype), halo], axis=0)
    return pl.pallas_call(
        conv_kernel,
        grid=(width // block,),
        in_specs=[
            pl.BlockSpec((8, block), lambda j: (0, j)),
            pl.BlockSpec((rows, block), lambda j: (0, j)),
            pl.BlockSpec((CONV, block), lambda j: (0, j)),
            pl.BlockSpec((1, block), lambda j: (0, j)),
        ],
        out_specs=pl.BlockSpec((rows, block), lambda j: (0, j)),
        out_shape=jax.ShapeDtypeStruct((rows, width), jnp.bfloat16),
        scratch_shapes=[pltpu.VMEM((rows + 8, block), jnp.float32)],
    )(halo8, x, weight, bias.reshape(1, width))

def block_parts(inner_block, b_block, c_block, step_sizes, log_rates):
    length = inner_block.shape[0]
    cumulative = jnp.cumsum(log_rates, axis=0)
    along = jnp.transpose(cumulative, (1, 2, 0))
    causal = lax.broadcasted_iota(jnp.int32, (length, length), 0) >= lax.broadcasted_iota(
        jnp.int32, (length, length), 1
    )
    decays = jnp.exp(jnp.where(causal, along[:, :, :, None] - along[:, :, None, :], -jnp.inf))
    scores = jnp.einsum("ign,jgn->gij", c_block, b_block, preferred_element_type=jnp.float32)
    mixing = (
        decays * scores[:, None] * jnp.transpose(step_sizes, (1, 2, 0))[:, :, None, :]
    ).astype(jnp.bfloat16)
    diagonal = jnp.einsum(
        "ghij,jghp->ighp", mixing, inner_block, preferred_element_type=jnp.float32
    )
    tail_weight = jnp.exp(cumulative[-1][None] - cumulative) * step_sizes
    weighted = (inner_block * tail_weight[..., None]).astype(jnp.bfloat16)
    block_state = jnp.einsum(
        "jghp,jgn->ghpn", weighted, b_block, preferred_element_type=jnp.float32
    )
    return diagonal, cumulative, block_state


def apply_state(c_block, state, cumulative):
    return jnp.exp(cumulative)[..., None] * jnp.einsum(
        "ign,ghpn->ighp", c_block.astype(jnp.float32), state, precision=lax.Precision.HIGHEST
    )


def block_local(carried_in, inputs_block):
    local_state, entry_total = carried_in
    inner_block, b_block, c_block, step_sizes, log_rates = inputs_block
    diagonal, cumulative, block_state = block_parts(*inputs_block)
    carried = apply_state(c_block, local_state, cumulative)
    new_state = jnp.exp(cumulative[-1])[..., None, None] * local_state + block_state
    return (
        (new_state, entry_total + cumulative[-1]),
        (diagonal + carried, cumulative + entry_total[None]),
    )


def pack(weight, state):
    rows = state.reshape(-1, state.shape[-1])
    high = weight.astype(jnp.bfloat16)
    low = (weight - high.astype(jnp.float32)).astype(jnp.bfloat16)
    lanes = rows.shape[-1]
    flat = jnp.concatenate([high.reshape(-1), low.reshape(-1)])
    pad = (-flat.shape[0]) % (16 * lanes)
    tail = jnp.pad(flat, (0, pad)).reshape(-1, lanes)
    return jnp.concatenate([rows.astype(jnp.bfloat16), tail], axis=0)


def unpack(packed, weight_shape, state_shape):
    count = 1
    for size in state_shape[:-1]:
        count *= size
    state = packed[:count].astype(jnp.float32).reshape(state_shape)
    flat = packed[count:].reshape(-1).astype(jnp.float32)
    size = 1
    for s in weight_shape:
        size *= s
    weight = (flat[:size] + flat[size : 2 * size]).reshape(weight_shape)
    return weight, state


def entering_state(total, state, axis):
    count = lax.axis_size(axis)
    weight = jnp.exp(total)
    if count == 1:
        return jnp.zeros_like(state)
    own = pack(weight, state)
    near_w, near_s = unpack(shifted(own, axis, 1), weight.shape, state.shape)
    if count == 2:
        return near_s
    far_w, far_s = unpack(shifted(own, axis, 2), weight.shape, state.shape)
    state = near_w[..., None, None] * far_s + near_s
    weight = near_w * far_w
    span = 2
    while 2 * span < count:
        far_w, far_s = unpack(shifted(pack(weight, state), axis, span), weight.shape, state.shape)
        state = weight[..., None, None] * far_s + state
        weight = weight * far_w
        span *= 2
    far = shifted(state.astype(jnp.bfloat16), axis, span).astype(jnp.float32)
    return weight[..., None, None] * far + state


def body(
    inner_input,
    state_input,
    gate_input,
    step_logits,
    conv_inner,
    conv_states,
    bias_inner,
    bias_states,
    decay_log,
    skip_gain,
    norm_gain,
    out_weight,
):
    tokens = inner_input.shape[0]
    margin = CONV - 1
    inner_width = inner_input.shape[1]
    halo = jnp.concatenate(
        [inner_input[tokens - margin :], state_input[tokens - margin :].reshape(margin, -1)], axis=1
    )
    halo = shifted(halo, "ctx", 1)
    inner_conv = conv_silu_kernel(halo[:, :inner_width], inner_input, conv_inner, bias_inner)
    state_conv = conv_silu(
        jnp.concatenate([halo[:, inner_width:].reshape((margin,) + state_input.shape[1:]), state_input], axis=0),
        conv_states,
        bias_states,
        tokens,
    )
    groups_here = state_input.shape[2] // STATE
    per_group = SSM_HEAD_COUNT // GROUPS
    blocks = tokens // BLK
    step_sizes = jax.nn.softplus(step_logits)
    log_rates = -step_sizes * jnp.exp(decay_log)[None]
    c_all = state_conv[:, 1].reshape(blocks, BLK, groups_here, STATE)
    inputs_all = (
        inner_conv.reshape(blocks, BLK, groups_here, per_group, HEAD_DIM),
        state_conv[:, 0].reshape(blocks, BLK, groups_here, STATE),
        c_all,
        step_sizes.reshape(blocks, BLK, groups_here, per_group),
        log_rates.reshape(blocks, BLK, groups_here, per_group),
    )
    if blocks == 1:
        diagonal, cumulative, local_state = block_parts(*(x[0] for x in inputs_all))
        partial_heads = diagonal[None]
        factors = cumulative[None]
        device_total = cumulative[-1]
    else:
        start_state = jnp.zeros((groups_here, per_group, HEAD_DIM, STATE), jnp.float32)
        start_total = jnp.zeros((groups_here, per_group), jnp.float32)
        (local_state, device_total), (partial_heads, factors) = lax.scan(
            block_local, (start_state, start_total), inputs_all
        )
    state_in = entering_state(device_total, local_state, "ctx")
    correction = jax.vmap(apply_state, in_axes=(0, None, 0))(c_all, state_in, factors)
    width_here = groups_here * per_group * HEAD_DIM
    mixed_heads = (partial_heads + correction).reshape(tokens, width_here) + jnp.repeat(
        skip_gain, HEAD_DIM
    )[None] * inner_conv.astype(jnp.float32)
    gated_out = mixed_heads * jax.nn.silu(gate_input.astype(jnp.float32))
    grouped = gated_out.reshape(tokens, groups_here, width_here // groups_here)
    normed = grouped * lax.rsqrt(jnp.mean(grouped * grouped, axis=-1, keepdims=True) + epsilon)
    normed = (normed.reshape(tokens, width_here) * norm_gain.astype(jnp.float32)).astype(
        jnp.bfloat16
    )
    return reduce_rows(normed, out_weight)


def swap(value, axis):
    return lax.ppermute(value, axis, [(0, 1), (1, 0)])


def reduce_rows(normed, out_weight):
    tokens = normed.shape[0]
    outer = lax.axis_size("ty")
    inner = lax.axis_size("tc")
    piece = tokens // (outer * inner)
    ty = lax.axis_index("ty")
    tc = lax.axis_index("tc")

    def project(block):
        partial = jnp.dot(block, out_weight, preferred_element_type=jnp.float32)
        return partial.astype(jnp.bfloat16)

    if inner != 2:
        projected = project(normed).reshape(outer * inner, piece, -1)
        return lax.psum_scatter(projected, ("ty", "tc"), scatter_dimension=0, tiled=True)[0]
    other = 1 - tc
    width = out_weight.shape[1]
    chunks = 4 if width % (4 * 128) == 0 else 1
    step = width // chunks
    done = []
    for c in range(chunks):
        partial = jnp.dot(
            normed, out_weight[:, c * step : (c + 1) * step], preferred_element_type=jnp.float32
        ).astype(jnp.bfloat16)
        partial = partial.reshape(outer, inner, piece, step)
        sent = swap(lax.dynamic_index_in_dim(partial, other, 1, keepdims=False), "tc")
        half = lax.dynamic_index_in_dim(partial, tc, 1, keepdims=False).astype(jnp.float32)
        half = half + sent.astype(jnp.float32)
        if outer == 2:
            across = swap(
                lax.dynamic_index_in_dim(half, 1 - ty, 0, keepdims=False).astype(jnp.bfloat16), "ty"
            )
            mine = lax.dynamic_index_in_dim(half, ty, 0, keepdims=False)
            done.append((mine + across.astype(jnp.float32)).astype(jnp.bfloat16))
        else:
            done.append(
                lax.psum_scatter(half.astype(jnp.bfloat16), "ty", scatter_dimension=0, tiled=True)[0]
            )
    return jnp.concatenate(done, axis=1)


def solution(mesh):
    cores = 2
    split = Mesh(
        mesh.devices.reshape(mesh.shape["ctx"], mesh.shape["tp"] // cores, cores),
        ("ctx", "ty", "tc"),
    )
    tp = ("ty", "tc")
    placed = (
        P("ctx", tp),
        P("ctx", None, tp),
        P("ctx", tp),
        P("ctx", tp),
        P(None, tp),
        P(None, None, tp),
        P(tp),
        P(None, tp),
        P(tp),
        P(tp),
        P(tp),
        P(tp, None),
    )
    return jax.shard_map(
        body, mesh=split, in_specs=placed, out_specs=P(("ctx",) + tp, None), check_vma=False
    )
```

```python
import jax
import jax.numpy as jnp
from jax import lax
from jax.sharding import Mesh, PartitionSpec as P

SSM_HEAD_COUNT = 128
HEAD_DIM = 64
STATE = 128
GROUPS = 8
CONV = 4
BLK = 512


epsilon = 1e-05


def shifted(value, axis, by):
    names = axis if isinstance(axis, tuple) else (axis,)
    count = 1
    for name in names:
        count *= lax.axis_size(name)
    pairs = [(i, i + by) for i in range(count) if 0 <= i + by < count]
    return lax.ppermute(value, axis, pairs)


def conv_silu(padded, weight, offsets, row_count):
    summed = offsets.astype(jnp.float32)
    for k in range(CONV):
        summed = summed + weight[k].astype(jnp.float32) * padded[k : k + row_count].astype(
            jnp.float32
        )
    return lax.optimization_barrier(jax.nn.silu(summed).astype(jnp.bfloat16))


def block_parts(inner_block, b_block, c_block, step_sizes, log_rates):
    length = inner_block.shape[0]
    cumulative = jnp.cumsum(log_rates, axis=0)
    along = jnp.transpose(cumulative, (1, 2, 0))
    causal = lax.broadcasted_iota(jnp.int32, (length, length), 0) >= lax.broadcasted_iota(
        jnp.int32, (length, length), 1
    )
    decays = jnp.exp(jnp.where(causal, along[:, :, :, None] - along[:, :, None, :], -jnp.inf))
    scores = jnp.einsum("ign,jgn->gij", c_block, b_block, preferred_element_type=jnp.float32)
    mixing = (
        decays * scores[:, None] * jnp.transpose(step_sizes, (1, 2, 0))[:, :, None, :]
    ).astype(jnp.bfloat16)
    diagonal = jnp.einsum(
        "ghij,jghp->ighp", mixing, inner_block, preferred_element_type=jnp.float32
    )
    tail_weight = jnp.exp(cumulative[-1][None] - cumulative) * step_sizes
    weighted = (inner_block * tail_weight[..., None]).astype(jnp.bfloat16)
    block_state = jnp.einsum(
        "jghp,jgn->ghpn", weighted, b_block, preferred_element_type=jnp.float32
    )
    return diagonal, cumulative, block_state


def apply_state(c_block, state, cumulative):
    return jnp.exp(cumulative)[..., None] * jnp.einsum(
        "ign,ghpn->ighp", c_block.astype(jnp.float32), state, precision=lax.Precision.HIGHEST
    )


def block_local(carried_in, inputs_block):
    local_state, entry_total = carried_in
    inner_block, b_block, c_block, step_sizes, log_rates = inputs_block
    diagonal, cumulative, block_state = block_parts(*inputs_block)
    carried = apply_state(c_block, local_state, cumulative)
    new_state = jnp.exp(cumulative[-1])[..., None, None] * local_state + block_state
    return (
        (new_state, entry_total + cumulative[-1]),
        (diagonal + carried, cumulative + entry_total[None]),
    )


def pack(weight, state):
    rows = state.reshape(-1, state.shape[-1])
    high = weight.astype(jnp.bfloat16)
    low = (weight - high.astype(jnp.float32)).astype(jnp.bfloat16)
    lanes = rows.shape[-1]
    flat = jnp.concatenate([high.reshape(-1), low.reshape(-1)])
    pad = (-flat.shape[0]) % (16 * lanes)
    tail = jnp.pad(flat, (0, pad)).reshape(-1, lanes)
    return jnp.concatenate([rows.astype(jnp.bfloat16), tail], axis=0)


def unpack(packed, weight_shape, state_shape):
    count = 1
    for size in state_shape[:-1]:
        count *= size
    state = packed[:count].astype(jnp.float32).reshape(state_shape)
    flat = packed[count:].reshape(-1).astype(jnp.float32)
    size = 1
    for s in weight_shape:
        size *= s
    weight = (flat[:size] + flat[size : 2 * size]).reshape(weight_shape)
    return weight, state


def entering_state(weight, state, axis):
    count = lax.axis_size(axis)
    if count == 1:
        return jnp.zeros_like(state)
    own = pack(weight, state)
    near_w, near_s = unpack(shifted(own, axis, 1), weight.shape, state.shape)
    if count == 2:
        return near_s
    far_w, far_s = unpack(shifted(own, axis, 2), weight.shape, state.shape)
    state = near_w[..., None, None] * far_s + near_s
    weight = near_w * far_w
    span = 2
    while 2 * span < count:
        far_w, far_s = unpack(shifted(pack(weight, state), axis, span), weight.shape, state.shape)
        state = weight[..., None, None] * far_s + state
        weight = weight * far_w
        span *= 2
    far = shifted(state.astype(jnp.bfloat16), axis, span).astype(jnp.float32)
    return weight[..., None, None] * far + state


def entering_pairs(total, state, lo, hi):
    shape = state.shape
    heads = total.size
    half = heads // 2
    weight = jnp.exp(total).reshape(heads)
    state = state.reshape((heads,) + shape[-2:])
    first = lax.axis_index(lo) == 0
    mine_w = jnp.where(first, weight[:half], weight[half:])
    mine_s = jnp.where(first, state[:half], state[half:])
    other_w = jnp.where(first, weight[half:], weight[:half])
    other_s = jnp.where(first, state[half:], state[:half])
    got_w, got_s = unpack(swap(pack(other_w, other_s), lo), (half,), (half,) + shape[-2:])
    w_first = jnp.where(first, mine_w, got_w)
    s_first = jnp.where(first, mine_s, got_s)
    w_second = jnp.where(first, got_w, mine_w)
    s_second = jnp.where(first, got_s, mine_s)
    pair_w = w_first * w_second
    pair_s = w_second[:, None, None] * s_first + s_second
    at_first = entering_state(pair_w, pair_s, hi)
    at_second = w_first[:, None, None] * at_first + s_first
    keep = jnp.where(first, at_first, at_second)
    give = jnp.where(first, at_second, at_first)
    got = swap(give.astype(jnp.bfloat16), lo).astype(jnp.float32)
    lower = jnp.where(first, keep, got)
    upper = jnp.where(first, got, keep)
    return jnp.concatenate([lower, upper], axis=0).reshape(shape)


def body(
    inner_input,
    state_input,
    gate_input,
    step_logits,
    conv_inner,
    conv_states,
    bias_inner,
    bias_states,
    decay_log,
    skip_gain,
    norm_gain,
    out_weight,
):
    tokens = inner_input.shape[0]
    margin = CONV - 1
    inner_width = inner_input.shape[1]
    halo = jnp.concatenate(
        [inner_input[tokens - margin :], state_input[tokens - margin :].reshape(margin, -1)], axis=1
    )
    halo = shifted(halo, ("chi", "clo"), 1)
    inner_conv = conv_silu(
        jnp.concatenate([halo[:, :inner_width], inner_input], axis=0), conv_inner, bias_inner, tokens
    )
    state_conv = conv_silu(
        jnp.concatenate([halo[:, inner_width:].reshape((margin,) + state_input.shape[1:]), state_input], axis=0),
        conv_states,
        bias_states,
        tokens,
    )
    groups_here = state_input.shape[2] // STATE
    per_group = SSM_HEAD_COUNT // GROUPS
    blocks = tokens // BLK
    step_sizes = jax.nn.softplus(step_logits)
    log_rates = -step_sizes * jnp.exp(decay_log)[None]
    c_all = state_conv[:, 1].reshape(blocks, BLK, groups_here, STATE)
    inputs_all = (
        inner_conv.reshape(blocks, BLK, groups_here, per_group, HEAD_DIM),
        state_conv[:, 0].reshape(blocks, BLK, groups_here, STATE),
        c_all,
        step_sizes.reshape(blocks, BLK, groups_here, per_group),
        log_rates.reshape(blocks, BLK, groups_here, per_group),
    )
    if blocks == 1:
        diagonal, cumulative, local_state = block_parts(*(x[0] for x in inputs_all))
        partial_heads = diagonal[None]
        factors = cumulative[None]
        device_total = cumulative[-1]
    else:
        start_state = jnp.zeros((groups_here, per_group, HEAD_DIM, STATE), jnp.float32)
        start_total = jnp.zeros((groups_here, per_group), jnp.float32)
        (local_state, device_total), (partial_heads, factors) = lax.scan(
            block_local, (start_state, start_total), inputs_all
        )
    state_in = entering_pairs(device_total, local_state, "clo", "chi")
    correction = jax.vmap(apply_state, in_axes=(0, None, 0))(c_all, state_in, factors)
    width_here = groups_here * per_group * HEAD_DIM
    mixed_heads = (partial_heads + correction).reshape(tokens, width_here) + jnp.repeat(
        skip_gain, HEAD_DIM
    )[None] * inner_conv.astype(jnp.float32)
    gated_out = mixed_heads * jax.nn.silu(gate_input.astype(jnp.float32))
    grouped = gated_out.reshape(tokens, groups_here, width_here // groups_here)
    normed = grouped * lax.rsqrt(jnp.mean(grouped * grouped, axis=-1, keepdims=True) + epsilon)
    normed = (normed.reshape(tokens, width_here) * norm_gain.astype(jnp.float32)).astype(
        jnp.bfloat16
    )
    return reduce_rows(normed, out_weight)


def swap(value, axis):
    return lax.ppermute(value, axis, [(0, 1), (1, 0)])


def reduce_rows(normed, out_weight):
    tokens = normed.shape[0]
    outer = lax.axis_size("ty")
    inner = lax.axis_size("tc")
    piece = tokens // (outer * inner)
    ty = lax.axis_index("ty")
    tc = lax.axis_index("tc")

    def project(block):
        partial = jnp.dot(block, out_weight, preferred_element_type=jnp.float32)
        return partial.astype(jnp.bfloat16)

    if inner != 2:
        projected = project(normed).reshape(outer * inner, piece, -1)
        return lax.psum_scatter(projected, ("ty", "tc"), scatter_dimension=0, tiled=True)[0]
    other = 1 - tc
    width = out_weight.shape[1]
    chunks = 4 if width % (4 * 128) == 0 else 1
    step = width // chunks
    done = []
    for c in range(chunks):
        partial = jnp.dot(
            normed, out_weight[:, c * step : (c + 1) * step], preferred_element_type=jnp.float32
        ).astype(jnp.bfloat16)
        partial = partial.reshape(outer, inner, piece, step)
        sent = swap(lax.dynamic_index_in_dim(partial, other, 1, keepdims=False), "tc")
        half = lax.dynamic_index_in_dim(partial, tc, 1, keepdims=False).astype(jnp.float32)
        half = half + sent.astype(jnp.float32)
        if outer == 2:
            across = swap(
                lax.dynamic_index_in_dim(half, 1 - ty, 0, keepdims=False).astype(jnp.bfloat16), "ty"
            )
            mine = lax.dynamic_index_in_dim(half, ty, 0, keepdims=False)
            done.append((mine + across.astype(jnp.float32)).astype(jnp.bfloat16))
        else:
            done.append(
                lax.psum_scatter(half.astype(jnp.bfloat16), "ty", scatter_dimension=0, tiled=True)[0]
            )
    return jnp.concatenate(done, axis=1)


def solution(mesh):
    cores = 2
    split = Mesh(
        mesh.devices.reshape(mesh.shape["ctx"] // 2, 2, mesh.shape["tp"] // cores, cores),
        ("chi", "clo", "ty", "tc"),
    )
    tp = ("ty", "tc")
    ctx = ("chi", "clo")
    placed = (
        P(ctx, tp),
        P(ctx, None, tp),
        P(ctx, tp),
        P(ctx, tp),
        P(None, tp),
        P(None, None, tp),
        P(tp),
        P(None, tp),
        P(tp),
        P(tp),
        P(tp),
        P(tp, None),
    )
    return jax.shard_map(
        body, mesh=split, in_specs=placed, out_specs=P(ctx + tp, None), check_vma=False
    )
```

```python
import jax
import jax.numpy as jnp
from jax import lax
from jax.sharding import Mesh, PartitionSpec as P

SSM_HEAD_COUNT = 128
HEAD_DIM = 64
STATE = 128
GROUPS = 8
CONV = 4
BLK = 512


epsilon = 1e-05


def shifted(value, axis, by):
    names = axis if isinstance(axis, tuple) else (axis,)
    count = 1
    for name in names:
        count *= lax.axis_size(name)
    pairs = [(i, i + by) for i in range(count) if 0 <= i + by < count]
    return lax.ppermute(value, axis, pairs)


def conv_silu(padded, weight, offsets, row_count):
    summed = offsets.astype(jnp.float32)
    for k in range(CONV):
        summed = summed + weight[k].astype(jnp.float32) * padded[k : k + row_count].astype(
            jnp.float32
        )
    return lax.optimization_barrier(jax.nn.silu(summed).astype(jnp.bfloat16))


def diagonal_of(inner_block, b_block, c_block, step_sizes, cumulative):
    length = inner_block.shape[0]
    along = jnp.transpose(cumulative, (1, 2, 0))
    causal = lax.broadcasted_iota(jnp.int32, (length, length), 0) >= lax.broadcasted_iota(
        jnp.int32, (length, length), 1
    )
    decays = jnp.exp(jnp.where(causal, along[:, :, :, None] - along[:, :, None, :], -jnp.inf))
    scores = jnp.einsum("ign,jgn->gij", c_block, b_block, preferred_element_type=jnp.float32)
    mixing = (
        decays * scores[:, None] * jnp.transpose(step_sizes, (1, 2, 0))[:, :, None, :]
    ).astype(jnp.bfloat16)
    return jnp.einsum("ghij,jghp->ighp", mixing, inner_block, preferred_element_type=jnp.float32)


def state_of(inner_block, b_block, step_sizes, cumulative):
    tail_weight = jnp.exp(cumulative[-1][None] - cumulative) * step_sizes
    weighted = (inner_block * tail_weight[..., None]).astype(jnp.bfloat16)
    return jnp.einsum("jghp,jgn->ghpn", weighted, b_block, preferred_element_type=jnp.float32)


def block_parts(inner_block, b_block, c_block, step_sizes, log_rates):
    cumulative = jnp.cumsum(log_rates, axis=0)
    diagonal = diagonal_of(inner_block, b_block, c_block, step_sizes, cumulative)
    block_state = state_of(inner_block, b_block, step_sizes, cumulative)
    return diagonal, cumulative, block_state


def apply_state(c_block, state, cumulative):
    return jnp.exp(cumulative)[..., None] * jnp.einsum(
        "ign,ghpn->ighp", c_block.astype(jnp.float32), state, precision=lax.Precision.HIGHEST
    )


def block_local(carried_in, inputs_block):
    local_state, entry_total = carried_in
    inner_block, b_block, c_block, step_sizes, log_rates = inputs_block
    diagonal, cumulative, block_state = block_parts(*inputs_block)
    carried = apply_state(c_block, local_state, cumulative)
    new_state = jnp.exp(cumulative[-1])[..., None, None] * local_state + block_state
    return (
        (new_state, entry_total + cumulative[-1]),
        (diagonal + carried, cumulative + entry_total[None]),
    )


def pack(weight, state):
    rows = state.reshape(-1, state.shape[-1])
    high = weight.astype(jnp.bfloat16)
    low = (weight - high.astype(jnp.float32)).astype(jnp.bfloat16)
    lanes = rows.shape[-1]
    flat = jnp.concatenate([high.reshape(-1), low.reshape(-1)])
    pad = (-flat.shape[0]) % (16 * lanes)
    tail = jnp.pad(flat, (0, pad)).reshape(-1, lanes)
    return jnp.concatenate([rows.astype(jnp.bfloat16), tail], axis=0)


def unpack(packed, weight_shape, state_shape):
    count = 1
    for size in state_shape[:-1]:
        count *= size
    state = packed[:count].astype(jnp.float32).reshape(state_shape)
    flat = packed[count:].reshape(-1).astype(jnp.float32)
    size = 1
    for s in weight_shape:
        size *= s
    weight = (flat[:size] + flat[size : 2 * size]).reshape(weight_shape)
    return weight, state


def entering_state(weight, state, axis, work=None, work_inputs=()):
    count = lax.axis_size(axis)
    if count == 1:
        return jnp.zeros_like(state), run(work, work_inputs)
    own = pack(weight, state)
    if count == 2:
        return unpack(shifted(own, axis, 1), weight.shape, state.shape)[1], run(work, work_inputs)
    near_w, near_s = unpack(shifted(own, axis, 1), weight.shape, state.shape)
    far_w, far_s = unpack(shifted(own, axis, 2), weight.shape, state.shape)
    state = near_w[..., None, None] * far_s + near_s
    weight = near_w * far_w
    span = 2
    while 2 * span < count:
        far_w, far_s = unpack(shifted(pack(weight, state), axis, span), weight.shape, state.shape)
        state = weight[..., None, None] * far_s + state
        weight = weight * far_w
        span *= 2
    payload = state.astype(jnp.bfloat16)
    if work is not None:
        payload, work_inputs = lax.optimization_barrier((payload, work_inputs))
    far = shifted(payload, axis, span)
    done = run(work, work_inputs)
    if work is not None:
        far, done = lax.optimization_barrier((far, done))
    return weight[..., None, None] * far.astype(jnp.float32) + state, done


def run(work, work_inputs):
    return None if work is None else work(*work_inputs)


def entering_pairs(total, state, lo, hi, work=None, work_inputs=()):
    shape = state.shape
    heads = total.size
    half = heads // 2
    weight = jnp.exp(total).reshape(heads)
    state = state.reshape((heads,) + shape[-2:])
    first = lax.axis_index(lo) == 0
    mine_w = jnp.where(first, weight[:half], weight[half:])
    mine_s = jnp.where(first, state[:half], state[half:])
    other_w = jnp.where(first, weight[half:], weight[:half])
    other_s = jnp.where(first, state[half:], state[:half])
    got_w, got_s = unpack(swap(pack(other_w, other_s), lo), (half,), (half,) + shape[-2:])
    w_first = jnp.where(first, mine_w, got_w)
    s_first = jnp.where(first, mine_s, got_s)
    w_second = jnp.where(first, got_w, mine_w)
    s_second = jnp.where(first, got_s, mine_s)
    pair_w = w_first * w_second
    pair_s = w_second[:, None, None] * s_first + s_second
    at_first, done = entering_state(pair_w, pair_s, hi, work, work_inputs)
    at_second = w_first[:, None, None] * at_first + s_first
    keep = jnp.where(first, at_first, at_second)
    give = jnp.where(first, at_second, at_first)
    got = swap(give.astype(jnp.bfloat16), lo).astype(jnp.float32)
    lower = jnp.where(first, keep, got)
    upper = jnp.where(first, got, keep)
    return jnp.concatenate([lower, upper], axis=0).reshape(shape), done


def body(
    inner_input,
    state_input,
    gate_input,
    step_logits,
    conv_inner,
    conv_states,
    bias_inner,
    bias_states,
    decay_log,
    skip_gain,
    norm_gain,
    out_weight,
):
    tokens = inner_input.shape[0]
    margin = CONV - 1
    inner_width = inner_input.shape[1]
    halo = jnp.concatenate(
        [inner_input[tokens - margin :], state_input[tokens - margin :].reshape(margin, -1)], axis=1
    )
    halo = shifted(halo, ("chi", "clo"), 1)
    inner_conv = conv_silu(
        jnp.concatenate([halo[:, :inner_width], inner_input], axis=0), conv_inner, bias_inner, tokens
    )
    state_conv = conv_silu(
        jnp.concatenate([halo[:, inner_width:].reshape((margin,) + state_input.shape[1:]), state_input], axis=0),
        conv_states,
        bias_states,
        tokens,
    )
    groups_here = state_input.shape[2] // STATE
    per_group = SSM_HEAD_COUNT // GROUPS
    blocks = tokens // BLK
    step_sizes = jax.nn.softplus(step_logits)
    log_rates = -step_sizes * jnp.exp(decay_log)[None]
    c_all = state_conv[:, 1].reshape(blocks, BLK, groups_here, STATE)
    inputs_all = (
        inner_conv.reshape(blocks, BLK, groups_here, per_group, HEAD_DIM),
        state_conv[:, 0].reshape(blocks, BLK, groups_here, STATE),
        c_all,
        step_sizes.reshape(blocks, BLK, groups_here, per_group),
        log_rates.reshape(blocks, BLK, groups_here, per_group),
    )
    if blocks == 1:
        inner_block, b_block, c_block, step_block, rate_block = (x[0] for x in inputs_all)
        cumulative = jnp.cumsum(rate_block, axis=0)
        local_state = state_of(inner_block, b_block, step_block, cumulative)
        state_in, diagonal = entering_pairs(
            cumulative[-1],
            local_state,
            "clo",
            "chi",
            lambda x, b, c: diagonal_of(x, b, c, step_block, cumulative),
            (inner_block, b_block, c_block),
        )
        partial_heads = diagonal[None]
        factors = cumulative[None]
    else:
        start_state = jnp.zeros((groups_here, per_group, HEAD_DIM, STATE), jnp.float32)
        start_total = jnp.zeros((groups_here, per_group), jnp.float32)
        (local_state, device_total), (partial_heads, factors) = lax.scan(
            block_local, (start_state, start_total), inputs_all
        )
        state_in = entering_pairs(device_total, local_state, "clo", "chi")[0]
    correction = jax.vmap(apply_state, in_axes=(0, None, 0))(c_all, state_in, factors)
    width_here = groups_here * per_group * HEAD_DIM
    mixed_heads = (partial_heads + correction).reshape(tokens, width_here) + jnp.repeat(
        skip_gain, HEAD_DIM
    )[None] * inner_conv.astype(jnp.float32)
    gated_out = mixed_heads * jax.nn.silu(gate_input.astype(jnp.float32))
    grouped = gated_out.reshape(tokens, groups_here, width_here // groups_here)
    normed = grouped * lax.rsqrt(jnp.mean(grouped * grouped, axis=-1, keepdims=True) + epsilon)
    normed = (normed.reshape(tokens, width_here) * norm_gain.astype(jnp.float32)).astype(
        jnp.bfloat16
    )
    return reduce_rows(normed, out_weight)


def swap(value, axis):
    return lax.ppermute(value, axis, [(0, 1), (1, 0)])


def reduce_rows(normed, out_weight):
    tokens = normed.shape[0]
    outer = lax.axis_size("ty")
    inner = lax.axis_size("tc")
    piece = tokens // (outer * inner)
    ty = lax.axis_index("ty")
    tc = lax.axis_index("tc")

    def project(block):
        partial = jnp.dot(block, out_weight, preferred_element_type=jnp.float32)
        return partial.astype(jnp.bfloat16)

    if inner != 2:
        projected = project(normed).reshape(outer * inner, piece, -1)
        return lax.psum_scatter(projected, ("ty", "tc"), scatter_dimension=0, tiled=True)[0]
    other = 1 - tc
    width = out_weight.shape[1]
    chunks = 4 if width % (4 * 128) == 0 else 1
    step = width // chunks
    done = []
    for c in range(chunks):
        partial = jnp.dot(
            normed, out_weight[:, c * step : (c + 1) * step], preferred_element_type=jnp.float32
        ).astype(jnp.bfloat16)
        partial = partial.reshape(outer, inner, piece, step)
        sent = swap(lax.dynamic_index_in_dim(partial, other, 1, keepdims=False), "tc")
        half = lax.dynamic_index_in_dim(partial, tc, 1, keepdims=False).astype(jnp.float32)
        half = half + sent.astype(jnp.float32)
        if outer == 2:
            across = swap(
                lax.dynamic_index_in_dim(half, 1 - ty, 0, keepdims=False).astype(jnp.bfloat16), "ty"
            )
            mine = lax.dynamic_index_in_dim(half, ty, 0, keepdims=False)
            done.append((mine + across.astype(jnp.float32)).astype(jnp.bfloat16))
        else:
            done.append(
                lax.psum_scatter(half.astype(jnp.bfloat16), "ty", scatter_dimension=0, tiled=True)[0]
            )
    return jnp.concatenate(done, axis=1)


def solution(mesh):
    cores = 2
    split = Mesh(
        mesh.devices.reshape(mesh.shape["ctx"] // 2, 2, mesh.shape["tp"] // cores, cores),
        ("chi", "clo", "ty", "tc"),
    )
    tp = ("ty", "tc")
    ctx = ("chi", "clo")
    placed = (
        P(ctx, tp),
        P(ctx, None, tp),
        P(ctx, tp),
        P(ctx, tp),
        P(None, tp),
        P(None, None, tp),
        P(tp),
        P(None, tp),
        P(tp),
        P(tp),
        P(tp),
        P(tp, None),
    )
    return jax.shard_map(
        body, mesh=split, in_specs=placed, out_specs=P(ctx + tp, None), check_vma=False
    )
```

```python
import jax
import jax.numpy as jnp
from jax import lax
from jax.experimental import pallas as pl
from jax.experimental.pallas import tpu as pltpu
from jax.sharding import Mesh, PartitionSpec as P

SSM_HEAD_COUNT = 128
HEAD_DIM = 64
STATE = 128
GROUPS = 8
CONV = 4
BLK = 512


epsilon = 1e-05


def shifted(value, axis, by):
    names = axis if isinstance(axis, tuple) else (axis,)
    count = 1
    for name in names:
        count *= lax.axis_size(name)
    pairs = [(i, i + by) for i in range(count) if 0 <= i + by < count]
    return lax.ppermute(value, axis, pairs)


def conv_silu(padded, weight, offsets, row_count):
    summed = offsets.astype(jnp.float32)
    for k in range(CONV):
        summed = summed + weight[k].astype(jnp.float32) * padded[k : k + row_count].astype(
            jnp.float32
        )
    return lax.optimization_barrier(jax.nn.silu(summed).astype(jnp.bfloat16))


def conv_kernel(halo_ref, x_ref, w_ref, b_ref, o_ref, pad_ref):
    rows = x_ref.shape[0]
    pad_ref[0:8, :] = halo_ref[...].astype(jnp.float32)
    pad_ref[8 : 8 + rows, :] = x_ref[...].astype(jnp.float32)
    summed = b_ref[...].astype(jnp.float32)
    for k in range(CONV):
        summed = summed + w_ref[k : k + 1, :].astype(jnp.float32) * pad_ref[8 - (CONV - 1) + k : 8 - (CONV - 1) + k + rows, :]
    o_ref[...] = jnp.transpose(jax.nn.silu(summed)).astype(o_ref.dtype)

def conv_silu_kernel(halo, x, weight, bias):
    rows, width = x.shape
    block = 512 if width % 512 == 0 else width
    halo8 = jnp.concatenate([jnp.zeros((8 - halo.shape[0], width), halo.dtype), halo], axis=0)
    return pl.pallas_call(
        conv_kernel,
        grid=(width // block,),
        in_specs=[
            pl.BlockSpec((8, block), lambda j: (0, j)),
            pl.BlockSpec((rows, block), lambda j: (0, j)),
            pl.BlockSpec((CONV, block), lambda j: (0, j)),
            pl.BlockSpec((1, block), lambda j: (0, j)),
        ],
        out_specs=pl.BlockSpec((block, rows), lambda j: (j, 0)),
        out_shape=jax.ShapeDtypeStruct((width, rows), jnp.bfloat16),
        scratch_shapes=[pltpu.VMEM((rows + 8, block), jnp.float32)],
    )(halo8, x, weight, bias.reshape(1, width))

def block_parts(inner_block, b_block, c_block, step_sizes, log_rates):
    length = inner_block.shape[0]
    cumulative = jnp.cumsum(log_rates, axis=0)
    along = jnp.transpose(cumulative, (1, 2, 0))
    causal = lax.broadcasted_iota(jnp.int32, (length, length), 0) >= lax.broadcasted_iota(
        jnp.int32, (length, length), 1
    )
    decays = jnp.exp(jnp.where(causal, along[:, :, :, None] - along[:, :, None, :], -jnp.inf))
    scores = jnp.einsum("ign,jgn->gij", c_block, b_block, preferred_element_type=jnp.float32)
    mixing = (
        decays * scores[:, None] * jnp.transpose(step_sizes, (1, 2, 0))[:, :, None, :]
    ).astype(jnp.bfloat16)
    diagonal = jnp.einsum(
        "ghij,jghp->ighp", mixing, inner_block, preferred_element_type=jnp.float32
    )
    tail_weight = jnp.exp(cumulative[-1][None] - cumulative) * step_sizes
    weighted = (inner_block * tail_weight[..., None]).astype(jnp.bfloat16)
    block_state = jnp.einsum(
        "jghp,jgn->ghpn", weighted, b_block, preferred_element_type=jnp.float32
    )
    return diagonal, cumulative, block_state


def apply_state(c_block, state, cumulative):
    return jnp.exp(cumulative)[..., None] * jnp.einsum(
        "ign,ghpn->ighp", c_block.astype(jnp.float32), state, precision=lax.Precision.HIGHEST
    )


def block_local(carried_in, inputs_block):
    local_state, entry_total = carried_in
    inner_block, b_block, c_block, step_sizes, log_rates = inputs_block
    diagonal, cumulative, block_state = block_parts(*inputs_block)
    carried = apply_state(c_block, local_state, cumulative)
    new_state = jnp.exp(cumulative[-1])[..., None, None] * local_state + block_state
    return (
        (new_state, entry_total + cumulative[-1]),
        (diagonal + carried, cumulative + entry_total[None]),
    )


def pack(weight, state):
    rows = state.reshape(-1, state.shape[-1])
    high = weight.astype(jnp.bfloat16)
    low = (weight - high.astype(jnp.float32)).astype(jnp.bfloat16)
    lanes = rows.shape[-1]
    flat = jnp.concatenate([high.reshape(-1), low.reshape(-1)])
    pad = (-flat.shape[0]) % (16 * lanes)
    tail = jnp.pad(flat, (0, pad)).reshape(-1, lanes)
    return jnp.concatenate([rows.astype(jnp.bfloat16), tail], axis=0)


def unpack(packed, weight_shape, state_shape):
    count = 1
    for size in state_shape[:-1]:
        count *= size
    state = packed[:count].astype(jnp.float32).reshape(state_shape)
    flat = packed[count:].reshape(-1).astype(jnp.float32)
    size = 1
    for s in weight_shape:
        size *= s
    weight = (flat[:size] + flat[size : 2 * size]).reshape(weight_shape)
    return weight, state


def entering_state(weight, state, axis):
    count = lax.axis_size(axis)
    if count == 1:
        return jnp.zeros_like(state)
    own = pack(weight, state)
    near_w, near_s = unpack(shifted(own, axis, 1), weight.shape, state.shape)
    if count == 2:
        return near_s
    far_w, far_s = unpack(shifted(own, axis, 2), weight.shape, state.shape)
    state = near_w[..., None, None] * far_s + near_s
    weight = near_w * far_w
    span = 2
    while 2 * span < count:
        far_w, far_s = unpack(shifted(pack(weight, state), axis, span), weight.shape, state.shape)
        state = weight[..., None, None] * far_s + state
        weight = weight * far_w
        span *= 2
    far = shifted(state.astype(jnp.bfloat16), axis, span).astype(jnp.float32)
    return weight[..., None, None] * far + state


def entering_pairs(total, state, lo, hi):
    shape = state.shape
    heads = total.size
    half = heads // 2
    weight = jnp.exp(total).reshape(heads)
    state = state.reshape((heads,) + shape[-2:])
    first = lax.axis_index(lo) == 0
    mine_w = jnp.where(first, weight[:half], weight[half:])
    mine_s = jnp.where(first, state[:half], state[half:])
    other_w = jnp.where(first, weight[half:], weight[:half])
    other_s = jnp.where(first, state[half:], state[:half])
    got_w, got_s = unpack(swap(pack(other_w, other_s), lo), (half,), (half,) + shape[-2:])
    w_first = jnp.where(first, mine_w, got_w)
    s_first = jnp.where(first, mine_s, got_s)
    w_second = jnp.where(first, got_w, mine_w)
    s_second = jnp.where(first, got_s, mine_s)
    pair_w = w_first * w_second
    pair_s = w_second[:, None, None] * s_first + s_second
    at_first = entering_state(pair_w, pair_s, hi)
    at_second = w_first[:, None, None] * at_first + s_first
    keep = jnp.where(first, at_first, at_second)
    give = jnp.where(first, at_second, at_first)
    got = swap(give.astype(jnp.bfloat16), lo).astype(jnp.float32)
    lower = jnp.where(first, keep, got)
    upper = jnp.where(first, got, keep)
    return jnp.concatenate([lower, upper], axis=0).reshape(shape)


def body(
    inner_input,
    state_input,
    gate_input,
    step_logits,
    conv_inner,
    conv_states,
    bias_inner,
    bias_states,
    decay_log,
    skip_gain,
    norm_gain,
    out_weight,
):
    tokens = inner_input.shape[0]
    margin = CONV - 1
    inner_width = inner_input.shape[1]
    halo = jnp.concatenate(
        [inner_input[tokens - margin :], state_input[tokens - margin :].reshape(margin, -1)], axis=1
    )
    halo = shifted(halo, ("chi", "clo"), 1)
    inner_conv = jnp.transpose(
        conv_silu_kernel(halo[:, :inner_width], inner_input, conv_inner, bias_inner)
    )
    state_conv = conv_silu(
        jnp.concatenate([halo[:, inner_width:].reshape((margin,) + state_input.shape[1:]), state_input], axis=0),
        conv_states,
        bias_states,
        tokens,
    )
    groups_here = state_input.shape[2] // STATE
    per_group = SSM_HEAD_COUNT // GROUPS
    blocks = tokens // BLK
    step_sizes = jax.nn.softplus(step_logits)
    log_rates = -step_sizes * jnp.exp(decay_log)[None]
    c_all = state_conv[:, 1].reshape(blocks, BLK, groups_here, STATE)
    inputs_all = (
        inner_conv.reshape(blocks, BLK, groups_here, per_group, HEAD_DIM),
        state_conv[:, 0].reshape(blocks, BLK, groups_here, STATE),
        c_all,
        step_sizes.reshape(blocks, BLK, groups_here, per_group),
        log_rates.reshape(blocks, BLK, groups_here, per_group),
    )
    if blocks == 1:
        diagonal, cumulative, local_state = block_parts(*(x[0] for x in inputs_all))
        partial_heads = diagonal[None]
        factors = cumulative[None]
        device_total = cumulative[-1]
    else:
        start_state = jnp.zeros((groups_here, per_group, HEAD_DIM, STATE), jnp.float32)
        start_total = jnp.zeros((groups_here, per_group), jnp.float32)
        (local_state, device_total), (partial_heads, factors) = lax.scan(
            block_local, (start_state, start_total), inputs_all
        )
    state_in = entering_pairs(device_total, local_state, "clo", "chi")
    correction = jax.vmap(apply_state, in_axes=(0, None, 0))(c_all, state_in, factors)
    width_here = groups_here * per_group * HEAD_DIM
    mixed_heads = (partial_heads + correction).reshape(tokens, width_here) + jnp.repeat(
        skip_gain, HEAD_DIM
    )[None] * inner_conv.astype(jnp.float32)
    gated_out = mixed_heads * jax.nn.silu(gate_input.astype(jnp.float32))
    grouped = gated_out.reshape(tokens, groups_here, width_here // groups_here)
    normed = grouped * lax.rsqrt(jnp.mean(grouped * grouped, axis=-1, keepdims=True) + epsilon)
    normed = (normed.reshape(tokens, width_here) * norm_gain.astype(jnp.float32)).astype(
        jnp.bfloat16
    )
    return reduce_rows(normed, out_weight)


def swap(value, axis):
    return lax.ppermute(value, axis, [(0, 1), (1, 0)])


def reduce_rows(normed, out_weight):
    tokens = normed.shape[0]
    outer = lax.axis_size("ty")
    inner = lax.axis_size("tc")
    piece = tokens // (outer * inner)
    ty = lax.axis_index("ty")
    tc = lax.axis_index("tc")

    def project(block):
        partial = jnp.dot(block, out_weight, preferred_element_type=jnp.float32)
        return partial.astype(jnp.bfloat16)

    if inner != 2:
        projected = project(normed).reshape(outer * inner, piece, -1)
        return lax.psum_scatter(projected, ("ty", "tc"), scatter_dimension=0, tiled=True)[0]
    other = 1 - tc
    width = out_weight.shape[1]
    chunks = 4 if width % (4 * 128) == 0 else 1
    step = width // chunks
    done = []
    for c in range(chunks):
        partial = jnp.dot(
            normed, out_weight[:, c * step : (c + 1) * step], preferred_element_type=jnp.float32
        ).astype(jnp.bfloat16)
        partial = partial.reshape(outer, inner, piece, step)
        sent = swap(lax.dynamic_index_in_dim(partial, other, 1, keepdims=False), "tc")
        half = lax.dynamic_index_in_dim(partial, tc, 1, keepdims=False).astype(jnp.float32)
        half = half + sent.astype(jnp.float32)
        if outer == 2:
            across = swap(
                lax.dynamic_index_in_dim(half, 1 - ty, 0, keepdims=False).astype(jnp.bfloat16), "ty"
            )
            mine = lax.dynamic_index_in_dim(half, ty, 0, keepdims=False)
            done.append((mine + across.astype(jnp.float32)).astype(jnp.bfloat16))
        else:
            done.append(
                lax.psum_scatter(half.astype(jnp.bfloat16), "ty", scatter_dimension=0, tiled=True)[0]
            )
    return jnp.concatenate(done, axis=1)


def solution(mesh):
    cores = 2
    split = Mesh(
        mesh.devices.reshape(mesh.shape["ctx"] // 2, 2, mesh.shape["tp"] // cores, cores),
        ("chi", "clo", "ty", "tc"),
    )
    tp = ("ty", "tc")
    ctx = ("chi", "clo")
    placed = (
        P(ctx, tp),
        P(ctx, None, tp),
        P(ctx, tp),
        P(ctx, tp),
        P(None, tp),
        P(None, None, tp),
        P(tp),
        P(None, tp),
        P(tp),
        P(tp),
        P(tp),
        P(tp, None),
    )
    return jax.shard_map(
        body, mesh=split, in_specs=placed, out_specs=P(ctx + tp, None), check_vma=False
    )
```

```python
import jax
import jax.numpy as jnp
from jax import lax
from jax.experimental import pallas as pl
from jax.experimental.pallas import tpu as pltpu
from jax.sharding import Mesh, PartitionSpec as P

SSM_HEAD_COUNT = 128
HEAD_DIM = 64
STATE = 128
GROUPS = 8
CONV = 4
BLK = 512


epsilon = 1e-05


def shifted(value, axis, by):
    names = axis if isinstance(axis, tuple) else (axis,)
    count = 1
    for name in names:
        count *= lax.axis_size(name)
    pairs = [(i, i + by) for i in range(count) if 0 <= i + by < count]
    return lax.ppermute(value, axis, pairs)


def conv_silu(padded, weight, offsets, row_count):
    summed = offsets.astype(jnp.float32)
    for k in range(CONV):
        summed = summed + weight[k].astype(jnp.float32) * padded[k : k + row_count].astype(
            jnp.float32
        )
    return lax.optimization_barrier(jax.nn.silu(summed).astype(jnp.bfloat16))


def conv_kernel(halo_ref, x_ref, w_ref, b_ref, o_ref, pad_ref):
    rows = x_ref.shape[0]
    pad_ref[0:8, :] = halo_ref[...].astype(jnp.float32)
    pad_ref[8 : 8 + rows, :] = x_ref[...].astype(jnp.float32)
    summed = b_ref[...].astype(jnp.float32)
    for k in range(CONV):
        summed = summed + w_ref[k : k + 1, :].astype(jnp.float32) * pad_ref[8 - (CONV - 1) + k : 8 - (CONV - 1) + k + rows, :]
    o_ref[...] = jnp.transpose(jax.nn.silu(summed)).astype(o_ref.dtype)

def conv_silu_kernel(halo, x, weight, bias):
    rows, width = x.shape
    block = 512 if width % 512 == 0 else width
    halo8 = jnp.concatenate([jnp.zeros((8 - halo.shape[0], width), halo.dtype), halo], axis=0)
    return pl.pallas_call(
        conv_kernel,
        grid=(width // block,),
        in_specs=[
            pl.BlockSpec((8, block), lambda j: (0, j)),
            pl.BlockSpec((rows, block), lambda j: (0, j)),
            pl.BlockSpec((CONV, block), lambda j: (0, j)),
            pl.BlockSpec((1, block), lambda j: (0, j)),
        ],
        out_specs=pl.BlockSpec((block, rows), lambda j: (j, 0)),
        out_shape=jax.ShapeDtypeStruct((width, rows), jnp.bfloat16),
        scratch_shapes=[pltpu.VMEM((rows + 8, block), jnp.float32)],
    )(halo8, x, weight, bias.reshape(1, width))

def diagonal_of(inner_block, b_block, c_block, step_sizes, cumulative):
    length = inner_block.shape[0]
    along = jnp.transpose(cumulative, (1, 2, 0))
    causal = lax.broadcasted_iota(jnp.int32, (length, length), 0) >= lax.broadcasted_iota(
        jnp.int32, (length, length), 1
    )
    decays = jnp.exp(jnp.where(causal, along[:, :, :, None] - along[:, :, None, :], -jnp.inf))
    scores = jnp.einsum("ign,jgn->gij", c_block, b_block, preferred_element_type=jnp.float32)
    mixing = (
        decays * scores[:, None] * jnp.transpose(step_sizes, (1, 2, 0))[:, :, None, :]
    ).astype(jnp.bfloat16)
    return jnp.einsum("ghij,jghp->ighp", mixing, inner_block, preferred_element_type=jnp.float32)


def state_of(inner_block, b_block, step_sizes, cumulative):
    tail_weight = jnp.exp(cumulative[-1][None] - cumulative) * step_sizes
    weighted = (inner_block * tail_weight[..., None]).astype(jnp.bfloat16)
    return jnp.einsum("jghp,jgn->ghpn", weighted, b_block, preferred_element_type=jnp.float32)


def block_parts(inner_block, b_block, c_block, step_sizes, log_rates):
    cumulative = jnp.cumsum(log_rates, axis=0)
    diagonal = diagonal_of(inner_block, b_block, c_block, step_sizes, cumulative)
    block_state = state_of(inner_block, b_block, step_sizes, cumulative)
    return diagonal, cumulative, block_state


def apply_state(c_block, state, cumulative):
    return jnp.exp(cumulative)[..., None] * jnp.einsum(
        "ign,ghpn->ighp", c_block.astype(jnp.float32), state, precision=lax.Precision.HIGHEST
    )


def block_local(carried_in, inputs_block):
    local_state, entry_total = carried_in
    inner_block, b_block, c_block, step_sizes, log_rates = inputs_block
    diagonal, cumulative, block_state = block_parts(*inputs_block)
    carried = apply_state(c_block, local_state, cumulative)
    new_state = jnp.exp(cumulative[-1])[..., None, None] * local_state + block_state
    return (
        (new_state, entry_total + cumulative[-1]),
        (diagonal + carried, cumulative + entry_total[None]),
    )


def pack(weight, state):
    rows = state.reshape(-1, state.shape[-1])
    high = weight.astype(jnp.bfloat16)
    low = (weight - high.astype(jnp.float32)).astype(jnp.bfloat16)
    lanes = rows.shape[-1]
    flat = jnp.concatenate([high.reshape(-1), low.reshape(-1)])
    pad = (-flat.shape[0]) % (16 * lanes)
    tail = jnp.pad(flat, (0, pad)).reshape(-1, lanes)
    return jnp.concatenate([rows.astype(jnp.bfloat16), tail], axis=0)


def unpack(packed, weight_shape, state_shape):
    count = 1
    for size in state_shape[:-1]:
        count *= size
    state = packed[:count].astype(jnp.float32).reshape(state_shape)
    flat = packed[count:].reshape(-1).astype(jnp.float32)
    size = 1
    for s in weight_shape:
        size *= s
    weight = (flat[:size] + flat[size : 2 * size]).reshape(weight_shape)
    return weight, state


def entering_state(weight, state, axis, work=None, work_inputs=()):
    count = lax.axis_size(axis)
    if count == 1:
        return jnp.zeros_like(state), run(work, work_inputs)
    own = pack(weight, state)
    if count == 2:
        return unpack(shifted(own, axis, 1), weight.shape, state.shape)[1], run(work, work_inputs)
    near_w, near_s = unpack(shifted(own, axis, 1), weight.shape, state.shape)
    far_w, far_s = unpack(shifted(own, axis, 2), weight.shape, state.shape)
    state = near_w[..., None, None] * far_s + near_s
    weight = near_w * far_w
    span = 2
    while 2 * span < count:
        far_w, far_s = unpack(shifted(pack(weight, state), axis, span), weight.shape, state.shape)
        state = weight[..., None, None] * far_s + state
        weight = weight * far_w
        span *= 2
    payload = state.astype(jnp.bfloat16)
    if work is not None:
        payload, work_inputs = lax.optimization_barrier((payload, work_inputs))
    far = shifted(payload, axis, span)
    done = run(work, work_inputs)
    if work is not None:
        far, done = lax.optimization_barrier((far, done))
    return weight[..., None, None] * far.astype(jnp.float32) + state, done


def run(work, work_inputs):
    return None if work is None else work(*work_inputs)


def entering_pairs(total, state, lo, hi, work=None, work_inputs=()):
    shape = state.shape
    heads = total.size
    half = heads // 2
    weight = jnp.exp(total).reshape(heads)
    state = state.reshape((heads,) + shape[-2:])
    first = lax.axis_index(lo) == 0
    mine_w = jnp.where(first, weight[:half], weight[half:])
    mine_s = jnp.where(first, state[:half], state[half:])
    other_w = jnp.where(first, weight[half:], weight[:half])
    other_s = jnp.where(first, state[half:], state[:half])
    got_w, got_s = unpack(swap(pack(other_w, other_s), lo), (half,), (half,) + shape[-2:])
    w_first = jnp.where(first, mine_w, got_w)
    s_first = jnp.where(first, mine_s, got_s)
    w_second = jnp.where(first, got_w, mine_w)
    s_second = jnp.where(first, got_s, mine_s)
    pair_w = w_first * w_second
    pair_s = w_second[:, None, None] * s_first + s_second
    at_first, done = entering_state(pair_w, pair_s, hi, work, work_inputs)
    at_second = w_first[:, None, None] * at_first + s_first
    keep = jnp.where(first, at_first, at_second)
    give = jnp.where(first, at_second, at_first)
    got = swap(give.astype(jnp.bfloat16), lo).astype(jnp.float32)
    lower = jnp.where(first, keep, got)
    upper = jnp.where(first, got, keep)
    return jnp.concatenate([lower, upper], axis=0).reshape(shape), done


def body(
    inner_input,
    state_input,
    gate_input,
    step_logits,
    conv_inner,
    conv_states,
    bias_inner,
    bias_states,
    decay_log,
    skip_gain,
    norm_gain,
    out_weight,
):
    tokens = inner_input.shape[0]
    margin = CONV - 1
    inner_width = inner_input.shape[1]
    halo = jnp.concatenate(
        [inner_input[tokens - margin :], state_input[tokens - margin :].reshape(margin, -1)], axis=1
    )
    halo = shifted(halo, ("chi", "clo"), 1)
    inner_conv = jnp.transpose(
        conv_silu_kernel(halo[:, :inner_width], inner_input, conv_inner, bias_inner)
    )
    state_conv = conv_silu(
        jnp.concatenate([halo[:, inner_width:].reshape((margin,) + state_input.shape[1:]), state_input], axis=0),
        conv_states,
        bias_states,
        tokens,
    )
    groups_here = state_input.shape[2] // STATE
    per_group = SSM_HEAD_COUNT // GROUPS
    blocks = tokens // BLK
    step_sizes = jax.nn.softplus(step_logits)
    log_rates = -step_sizes * jnp.exp(decay_log)[None]
    c_all = state_conv[:, 1].reshape(blocks, BLK, groups_here, STATE)
    inputs_all = (
        inner_conv.reshape(blocks, BLK, groups_here, per_group, HEAD_DIM),
        state_conv[:, 0].reshape(blocks, BLK, groups_here, STATE),
        c_all,
        step_sizes.reshape(blocks, BLK, groups_here, per_group),
        log_rates.reshape(blocks, BLK, groups_here, per_group),
    )
    if blocks == 1:
        inner_block, b_block, c_block, step_block, rate_block = (x[0] for x in inputs_all)
        cumulative = jnp.cumsum(rate_block, axis=0)
        local_state = state_of(inner_block, b_block, step_block, cumulative)
        state_in, diagonal = entering_pairs(
            cumulative[-1],
            local_state,
            "clo",
            "chi",
            lambda x, b, c: diagonal_of(x, b, c, step_block, cumulative),
            (inner_block, b_block, c_block),
        )
        partial_heads = diagonal[None]
        factors = cumulative[None]
    else:
        start_state = jnp.zeros((groups_here, per_group, HEAD_DIM, STATE), jnp.float32)
        start_total = jnp.zeros((groups_here, per_group), jnp.float32)
        (local_state, device_total), (partial_heads, factors) = lax.scan(
            block_local, (start_state, start_total), inputs_all
        )
        state_in = entering_pairs(device_total, local_state, "clo", "chi")[0]
    correction = jax.vmap(apply_state, in_axes=(0, None, 0))(c_all, state_in, factors)
    width_here = groups_here * per_group * HEAD_DIM
    mixed_heads = (partial_heads + correction).reshape(tokens, width_here) + jnp.repeat(
        skip_gain, HEAD_DIM
    )[None] * inner_conv.astype(jnp.float32)
    gated_out = mixed_heads * jax.nn.silu(gate_input.astype(jnp.float32))
    grouped = gated_out.reshape(tokens, groups_here, width_here // groups_here)
    normed = grouped * lax.rsqrt(jnp.mean(grouped * grouped, axis=-1, keepdims=True) + epsilon)
    normed = (normed.reshape(tokens, width_here) * norm_gain.astype(jnp.float32)).astype(
        jnp.bfloat16
    )
    return reduce_rows(normed, out_weight)


def swap(value, axis):
    return lax.ppermute(value, axis, [(0, 1), (1, 0)])


def reduce_rows(normed, out_weight):
    tokens = normed.shape[0]
    outer = lax.axis_size("ty")
    inner = lax.axis_size("tc")
    piece = tokens // (outer * inner)
    ty = lax.axis_index("ty")
    tc = lax.axis_index("tc")

    def project(block):
        partial = jnp.dot(block, out_weight, preferred_element_type=jnp.float32)
        return partial.astype(jnp.bfloat16)

    if inner != 2:
        projected = project(normed).reshape(outer * inner, piece, -1)
        return lax.psum_scatter(projected, ("ty", "tc"), scatter_dimension=0, tiled=True)[0]
    other = 1 - tc
    width = out_weight.shape[1]
    chunks = 4 if width % (4 * 128) == 0 else 1
    step = width // chunks
    done = []
    for c in range(chunks):
        partial = jnp.dot(
            normed, out_weight[:, c * step : (c + 1) * step], preferred_element_type=jnp.float32
        ).astype(jnp.bfloat16)
        partial = partial.reshape(outer, inner, piece, step)
        sent = swap(lax.dynamic_index_in_dim(partial, other, 1, keepdims=False), "tc")
        half = lax.dynamic_index_in_dim(partial, tc, 1, keepdims=False).astype(jnp.float32)
        half = half + sent.astype(jnp.float32)
        if outer == 2:
            across = swap(
                lax.dynamic_index_in_dim(half, 1 - ty, 0, keepdims=False).astype(jnp.bfloat16), "ty"
            )
            mine = lax.dynamic_index_in_dim(half, ty, 0, keepdims=False)
            done.append((mine + across.astype(jnp.float32)).astype(jnp.bfloat16))
        else:
            done.append(
                lax.psum_scatter(half.astype(jnp.bfloat16), "ty", scatter_dimension=0, tiled=True)[0]
            )
    return jnp.concatenate(done, axis=1)


def solution(mesh):
    cores = 2
    split = Mesh(
        mesh.devices.reshape(mesh.shape["ctx"] // 2, 2, mesh.shape["tp"] // cores, cores),
        ("chi", "clo", "ty", "tc"),
    )
    tp = ("ty", "tc")
    ctx = ("chi", "clo")
    placed = (
        P(ctx, tp),
        P(ctx, None, tp),
        P(ctx, tp),
        P(ctx, tp),
        P(None, tp),
        P(None, None, tp),
        P(tp),
        P(None, tp),
        P(tp),
        P(tp),
        P(tp),
        P(tp, None),
    )
    return jax.shard_map(
        body, mesh=split, in_specs=placed, out_specs=P(ctx + tp, None), check_vma=False
    )
```

```python
import jax
import jax.numpy as jnp
from jax import lax
from jax.experimental import pallas as pl
from jax.experimental.pallas import tpu as pltpu
from jax.sharding import Mesh, PartitionSpec as P

SSM_HEAD_COUNT = 128
HEAD_DIM = 64
STATE = 128
GROUPS = 8
CONV = 4
BLK = 512


epsilon = 1e-05


def shifted(value, axis, by):
    names = axis if isinstance(axis, tuple) else (axis,)
    count = 1
    for name in names:
        count *= lax.axis_size(name)
    pairs = [(i, i + by) for i in range(count) if 0 <= i + by < count]
    return lax.ppermute(value, axis, pairs)


def conv_silu(padded, weight, offsets, row_count):
    summed = offsets.astype(jnp.float32)
    for k in range(CONV):
        summed = summed + weight[k].astype(jnp.float32) * padded[k : k + row_count].astype(
            jnp.float32
        )
    return lax.optimization_barrier(jax.nn.silu(summed).astype(jnp.bfloat16))


def conv_kernel(halo_ref, x_ref, w_ref, b_ref, o_ref, pad_ref):
    rows = x_ref.shape[0]
    pad_ref[0:8, :] = halo_ref[...].astype(jnp.float32)
    pad_ref[8 : 8 + rows, :] = x_ref[...].astype(jnp.float32)
    summed = b_ref[...].astype(jnp.float32)
    for k in range(CONV):
        summed = summed + w_ref[k : k + 1, :].astype(jnp.float32) * pad_ref[8 - (CONV - 1) + k : 8 - (CONV - 1) + k + rows, :]
    o_ref[...] = jnp.transpose(jax.nn.silu(summed)).astype(o_ref.dtype)

def conv_silu_kernel(halo, x, weight, bias):
    rows, width = x.shape
    block = 512 if width % 512 == 0 else width
    halo8 = jnp.concatenate([jnp.zeros((8 - halo.shape[0], width), halo.dtype), halo], axis=0)
    return pl.pallas_call(
        conv_kernel,
        grid=(width // block,),
        in_specs=[
            pl.BlockSpec((8, block), lambda j: (0, j)),
            pl.BlockSpec((rows, block), lambda j: (0, j)),
            pl.BlockSpec((CONV, block), lambda j: (0, j)),
            pl.BlockSpec((1, block), lambda j: (0, j)),
        ],
        out_specs=pl.BlockSpec((block, rows), lambda j: (j, 0)),
        out_shape=jax.ShapeDtypeStruct((width, rows), jnp.bfloat16),
        scratch_shapes=[pltpu.VMEM((rows + 8, block), jnp.float32)],
    )(halo8, x, weight, bias.reshape(1, width))

def diagonal_of(inner_block, b_block, c_block, step_sizes, cumulative):
    length = inner_block.shape[0]
    along = jnp.transpose(cumulative, (1, 2, 0))
    causal = lax.broadcasted_iota(jnp.int32, (length, length), 0) >= lax.broadcasted_iota(
        jnp.int32, (length, length), 1
    )
    decays = jnp.exp(jnp.where(causal, along[:, :, :, None] - along[:, :, None, :], -jnp.inf))
    scores = jnp.einsum("ign,jgn->gij", c_block, b_block, preferred_element_type=jnp.float32)
    mixing = (
        decays * scores[:, None] * jnp.transpose(step_sizes, (1, 2, 0))[:, :, None, :]
    ).astype(jnp.bfloat16)
    return jnp.einsum("ghij,jghp->ighp", mixing, inner_block, preferred_element_type=jnp.float32)


def state_of(inner_block, b_block, step_sizes, cumulative):
    tail_weight = jnp.exp(cumulative[-1][None] - cumulative) * step_sizes
    weighted = (inner_block * tail_weight[..., None]).astype(jnp.bfloat16)
    return jnp.einsum("jghp,jgn->ghpn", weighted, b_block, preferred_element_type=jnp.float32)


def block_parts(inner_block, b_block, c_block, step_sizes, log_rates):
    cumulative = jnp.cumsum(log_rates, axis=0)
    diagonal = diagonal_of(inner_block, b_block, c_block, step_sizes, cumulative)
    block_state = state_of(inner_block, b_block, step_sizes, cumulative)
    return diagonal, cumulative, block_state


def apply_state(c_block, state, cumulative):
    return jnp.exp(cumulative)[..., None] * jnp.einsum(
        "ign,ghpn->ighp", c_block.astype(jnp.float32), state, precision=lax.Precision.HIGHEST
    )


def block_local(carried_in, inputs_block):
    local_state, entry_total = carried_in
    inner_block, b_block, c_block, step_sizes, log_rates = inputs_block
    diagonal, cumulative, block_state = block_parts(*inputs_block)
    carried = apply_state(c_block, local_state, cumulative)
    new_state = jnp.exp(cumulative[-1])[..., None, None] * local_state + block_state
    return (
        (new_state, entry_total + cumulative[-1]),
        (diagonal + carried, cumulative + entry_total[None]),
    )


def pack(weight, state):
    rows = state.reshape(-1, state.shape[-1])
    high = weight.astype(jnp.bfloat16)
    low = (weight - high.astype(jnp.float32)).astype(jnp.bfloat16)
    lanes = rows.shape[-1]
    flat = jnp.concatenate([high.reshape(-1), low.reshape(-1)])
    pad = (-flat.shape[0]) % (16 * lanes)
    tail = jnp.pad(flat, (0, pad)).reshape(-1, lanes)
    return jnp.concatenate([rows.astype(jnp.bfloat16), tail], axis=0)


def unpack(packed, weight_shape, state_shape):
    count = 1
    for size in state_shape[:-1]:
        count *= size
    state = packed[:count].astype(jnp.float32).reshape(state_shape)
    flat = packed[count:].reshape(-1).astype(jnp.float32)
    size = 1
    for s in weight_shape:
        size *= s
    weight = (flat[:size] + flat[size : 2 * size]).reshape(weight_shape)
    return weight, state


def entering_state(weight, state, axis, work=None, work_inputs=()):
    count = lax.axis_size(axis)
    if count == 1:
        return jnp.zeros_like(state), run(work, work_inputs)
    own = pack(weight, state)
    if count == 2:
        return unpack(shifted(own, axis, 1), weight.shape, state.shape)[1], run(work, work_inputs)
    near_w, near_s = unpack(shifted(own, axis, 1), weight.shape, state.shape)
    far_w, far_s = unpack(shifted(own, axis, 2), weight.shape, state.shape)
    state = near_w[..., None, None] * far_s + near_s
    weight = near_w * far_w
    span = 2
    while 2 * span < count:
        far_w, far_s = unpack(shifted(pack(weight, state), axis, span), weight.shape, state.shape)
        state = weight[..., None, None] * far_s + state
        weight = weight * far_w
        span *= 2
    payload = state.astype(jnp.bfloat16)
    if work is not None:
        payload, work_inputs = lax.optimization_barrier((payload, work_inputs))
    far = shifted(payload, axis, span)
    done = run(work, work_inputs)
    if work is not None:
        far, done = lax.optimization_barrier((far, done))
    return weight[..., None, None] * far.astype(jnp.float32) + state, done


def run(work, work_inputs):
    return None if work is None else work(*work_inputs)


def entering_pairs(total, state, lo, hi, work=None, work_inputs=()):
    shape = state.shape
    heads = total.size
    half = heads // 2
    weight = jnp.exp(total).reshape(heads)
    state = state.reshape((heads,) + shape[-2:])
    first = lax.axis_index(lo) == 0
    mine_w = jnp.where(first, weight[:half], weight[half:])
    mine_s = jnp.where(first, state[:half], state[half:])
    other_w = jnp.where(first, weight[half:], weight[:half])
    other_s = jnp.where(first, state[half:], state[:half])
    got_w, got_s = unpack(swap(pack(other_w, other_s), lo), (half,), (half,) + shape[-2:])
    w_first = jnp.where(first, mine_w, got_w)
    s_first = jnp.where(first, mine_s, got_s)
    w_second = jnp.where(first, got_w, mine_w)
    s_second = jnp.where(first, got_s, mine_s)
    pair_w = w_first * w_second
    pair_s = w_second[:, None, None] * s_first + s_second
    at_first, done = entering_state(pair_w, pair_s, hi, work, work_inputs)
    at_second = w_first[:, None, None] * at_first + s_first
    keep = jnp.where(first, at_first, at_second)
    give = jnp.where(first, at_second, at_first)
    got = swap(give.astype(jnp.bfloat16), lo).astype(jnp.float32)
    lower = jnp.where(first, keep, got)
    upper = jnp.where(first, got, keep)
    return jnp.concatenate([lower, upper], axis=0).reshape(shape), done


def body(
    inner_input,
    state_input,
    gate_input,
    step_logits,
    conv_inner,
    conv_states,
    bias_inner,
    bias_states,
    decay_log,
    skip_gain,
    norm_gain,
    out_weight,
):
    tokens = inner_input.shape[0]
    margin = CONV - 1
    inner_width = inner_input.shape[1]
    halo = jnp.concatenate(
        [inner_input[tokens - margin :], state_input[tokens - margin :].reshape(margin, -1)], axis=1
    )
    halo = shifted(halo, ("chi", "clo"), 1)
    inner_conv = jnp.transpose(
        conv_silu_kernel(halo[:, :inner_width], inner_input, conv_inner, bias_inner)
    )
    state_conv = conv_silu(
        jnp.concatenate([halo[:, inner_width:].reshape((margin,) + state_input.shape[1:]), state_input], axis=0),
        conv_states,
        bias_states,
        tokens,
    )
    groups_here = state_input.shape[2] // STATE
    per_group = SSM_HEAD_COUNT // GROUPS
    blocks = tokens // BLK
    step_sizes = jax.nn.softplus(step_logits)
    log_rates = -step_sizes * jnp.exp(decay_log)[None]
    c_all = state_conv[:, 1].reshape(blocks, BLK, groups_here, STATE)
    inputs_all = (
        inner_conv.reshape(blocks, BLK, groups_here, per_group, HEAD_DIM),
        state_conv[:, 0].reshape(blocks, BLK, groups_here, STATE),
        c_all,
        step_sizes.reshape(blocks, BLK, groups_here, per_group),
        log_rates.reshape(blocks, BLK, groups_here, per_group),
    )
    if blocks == 1:
        inner_block, b_block, c_block, step_block, rate_block = (x[0] for x in inputs_all)
        cumulative = jnp.cumsum(rate_block, axis=0)
        local_state = state_of(inner_block, b_block, step_block, cumulative)
        state_in, diagonal = entering_pairs(
            cumulative[-1],
            local_state,
            "clo",
            "chi",
            lambda x, b, c: diagonal_of(x, b, c, step_block, cumulative),
            (inner_block, b_block, c_block),
        )
        partial_heads = diagonal[None]
        factors = cumulative[None]
    else:
        start_state = jnp.zeros((groups_here, per_group, HEAD_DIM, STATE), jnp.float32)
        start_total = jnp.zeros((groups_here, per_group), jnp.float32)
        (local_state, device_total), (partial_heads, factors) = lax.scan(
            block_local, (start_state, start_total), inputs_all
        )
        state_in = entering_pairs(device_total, local_state, "clo", "chi")[0]
    correction = jax.vmap(apply_state, in_axes=(0, None, 0))(c_all, state_in, factors)
    width_here = groups_here * per_group * HEAD_DIM
    mixed_heads = (partial_heads + correction).reshape(tokens, width_here) + jnp.repeat(
        skip_gain, HEAD_DIM
    )[None] * inner_conv.astype(jnp.float32)
    gated_out = mixed_heads * jax.nn.silu(gate_input.astype(jnp.float32))
    grouped = gated_out.reshape(tokens, groups_here, width_here // groups_here)
    normed = grouped * lax.rsqrt(jnp.mean(grouped * grouped, axis=-1, keepdims=True) + epsilon)
    normed = (normed.reshape(tokens, width_here) * norm_gain.astype(jnp.float32)).astype(
        jnp.bfloat16
    )
    return reduce_rows(normed, out_weight)


def swap(value, axis):
    return lax.ppermute(value, axis, [(0, 1), (1, 0)])


def reduce_rows(normed, out_weight):
    tokens = normed.shape[0]
    outer = lax.axis_size("ty")
    inner = lax.axis_size("tc")
    piece = tokens // (outer * inner)
    ty = lax.axis_index("ty")
    tc = lax.axis_index("tc")

    def project(block):
        partial = jnp.dot(block, out_weight, preferred_element_type=jnp.float32)
        return partial.astype(jnp.bfloat16)

    if inner != 2:
        projected = project(normed).reshape(outer * inner, piece, -1)
        return lax.psum_scatter(projected, ("ty", "tc"), scatter_dimension=0, tiled=True)[0]
    other = 1 - tc
    width = out_weight.shape[1]
    chunks = 4 if width % (4 * 128) == 0 else 1
    step = width // chunks
    done = []
    payloads = []
    for c in range(chunks):
        source = normed
        if c == chunks - 1 and c > 0 and payloads[0] is not None:
            payloads[0], source = lax.optimization_barrier((payloads[0], normed))
        partial = jnp.dot(
            source, out_weight[:, c * step : (c + 1) * step], preferred_element_type=jnp.float32
        ).astype(jnp.bfloat16)
        partial = partial.reshape(outer, inner, piece, step)
        sent = swap(lax.dynamic_index_in_dim(partial, other, 1, keepdims=False), "tc")
        half = lax.dynamic_index_in_dim(partial, tc, 1, keepdims=False).astype(jnp.float32)
        half = half + sent.astype(jnp.float32)
        if outer == 2:
            payloads.append(
                lax.dynamic_index_in_dim(half, 1 - ty, 0, keepdims=False).astype(jnp.bfloat16)
            )
        else:
            payloads.append(None)
        done.append(half)
    for c in range(chunks):
        half = done[c]
        if outer == 2:
            across = swap(payloads[c], "ty")
            mine = lax.dynamic_index_in_dim(half, ty, 0, keepdims=False)
            done[c] = (mine + across.astype(jnp.float32)).astype(jnp.bfloat16)
        else:
            done[c] = lax.psum_scatter(
                half.astype(jnp.bfloat16), "ty", scatter_dimension=0, tiled=True
            )[0]
    return jnp.concatenate(done, axis=1)


def solution(mesh):
    cores = 2
    split = Mesh(
        mesh.devices.reshape(mesh.shape["ctx"] // 2, 2, mesh.shape["tp"] // cores, cores),
        ("chi", "clo", "ty", "tc"),
    )
    tp = ("ty", "tc")
    ctx = ("chi", "clo")
    placed = (
        P(ctx, tp),
        P(ctx, None, tp),
        P(ctx, tp),
        P(ctx, tp),
        P(None, tp),
        P(None, None, tp),
        P(tp),
        P(None, tp),
        P(tp),
        P(tp),
        P(tp),
        P(tp, None),
    )
    return jax.shard_map(
        body, mesh=split, in_specs=placed, out_specs=P(ctx + tp, None), check_vma=False
    )
```

```python
import jax
import jax.numpy as jnp
from jax import lax
from jax.experimental import pallas as pl
from jax.experimental.pallas import tpu as pltpu
from jax.sharding import Mesh, PartitionSpec as P

SSM_HEAD_COUNT = 128
HEAD_DIM = 64
STATE = 128
GROUPS = 8
CONV = 4
BLK = 512


epsilon = 1e-05


def shifted(value, axis, by):
    names = axis if isinstance(axis, tuple) else (axis,)
    count = 1
    for name in names:
        count *= lax.axis_size(name)
    pairs = [(i, i + by) for i in range(count) if 0 <= i + by < count]
    return lax.ppermute(value, axis, pairs)


def conv_silu(padded, weight, offsets, row_count):
    summed = offsets.astype(jnp.float32)
    for k in range(CONV):
        summed = summed + weight[k].astype(jnp.float32) * padded[k : k + row_count].astype(
            jnp.float32
        )
    return lax.optimization_barrier(jax.nn.silu(summed).astype(jnp.bfloat16))


def conv_kernel(halo_ref, x_ref, w_ref, b_ref, o_ref, pad_ref):
    rows = x_ref.shape[0]
    pad_ref[0:8, :] = halo_ref[...].astype(jnp.float32)
    pad_ref[8 : 8 + rows, :] = x_ref[...].astype(jnp.float32)
    summed = b_ref[...].astype(jnp.float32)
    for k in range(CONV):
        summed = summed + w_ref[k : k + 1, :].astype(jnp.float32) * pad_ref[8 - (CONV - 1) + k : 8 - (CONV - 1) + k + rows, :]
    o_ref[...] = jnp.transpose(jax.nn.silu(summed)).astype(o_ref.dtype)

def conv_silu_kernel(halo, x, weight, bias):
    rows, width = x.shape
    block = 512 if width % 512 == 0 else width
    halo8 = jnp.concatenate([jnp.zeros((8 - halo.shape[0], width), halo.dtype), halo], axis=0)
    return pl.pallas_call(
        conv_kernel,
        grid=(width // block,),
        in_specs=[
            pl.BlockSpec((8, block), lambda j: (0, j)),
            pl.BlockSpec((rows, block), lambda j: (0, j)),
            pl.BlockSpec((CONV, block), lambda j: (0, j)),
            pl.BlockSpec((1, block), lambda j: (0, j)),
        ],
        out_specs=pl.BlockSpec((block, rows), lambda j: (j, 0)),
        out_shape=jax.ShapeDtypeStruct((width, rows), jnp.bfloat16),
        scratch_shapes=[pltpu.VMEM((rows + 8, block), jnp.float32)],
    )(halo8, x, weight, bias.reshape(1, width))

def diagonal_of(inner_block, b_block, c_block, step_sizes, cumulative):
    length = inner_block.shape[0]
    along = jnp.transpose(cumulative, (1, 2, 0))
    causal = lax.broadcasted_iota(jnp.int32, (length, length), 0) >= lax.broadcasted_iota(
        jnp.int32, (length, length), 1
    )
    decays = jnp.exp(jnp.where(causal, along[:, :, :, None] - along[:, :, None, :], -jnp.inf))
    scores = jnp.einsum("ign,jgn->gij", c_block, b_block, preferred_element_type=jnp.float32)
    mixing = (
        decays * scores[:, None] * jnp.transpose(step_sizes, (1, 2, 0))[:, :, None, :]
    ).astype(jnp.bfloat16)
    return jnp.einsum("ghij,jghp->ighp", mixing, inner_block, preferred_element_type=jnp.float32)


def state_of(inner_block, b_block, step_sizes, cumulative):
    tail_weight = jnp.exp(cumulative[-1][None] - cumulative) * step_sizes
    weighted = (inner_block * tail_weight[..., None]).astype(jnp.bfloat16)
    return jnp.einsum("jghp,jgn->ghpn", weighted, b_block, preferred_element_type=jnp.float32)


def block_parts(inner_block, b_block, c_block, step_sizes, log_rates):
    cumulative = jnp.cumsum(log_rates, axis=0)
    diagonal = diagonal_of(inner_block, b_block, c_block, step_sizes, cumulative)
    block_state = state_of(inner_block, b_block, step_sizes, cumulative)
    return diagonal, cumulative, block_state


def apply_state(c_block, state, cumulative):
    return jnp.exp(cumulative)[..., None] * jnp.einsum(
        "ign,ghpn->ighp", c_block.astype(jnp.float32), state, precision=lax.Precision.HIGHEST
    )


def block_local(carried_in, inputs_block):
    local_state, entry_total = carried_in
    inner_block, b_block, c_block, step_sizes, log_rates = inputs_block
    diagonal, cumulative, block_state = block_parts(*inputs_block)
    carried = apply_state(c_block, local_state, cumulative)
    new_state = jnp.exp(cumulative[-1])[..., None, None] * local_state + block_state
    return (
        (new_state, entry_total + cumulative[-1]),
        (diagonal + carried, cumulative + entry_total[None]),
    )


def pack(weight, state):
    rows = state.reshape(-1, state.shape[-1])
    high = weight.astype(jnp.bfloat16)
    low = (weight - high.astype(jnp.float32)).astype(jnp.bfloat16)
    lanes = rows.shape[-1]
    flat = jnp.concatenate([high.reshape(-1), low.reshape(-1)])
    pad = (-flat.shape[0]) % (16 * lanes)
    tail = jnp.pad(flat, (0, pad)).reshape(-1, lanes)
    return jnp.concatenate([rows.astype(jnp.bfloat16), tail], axis=0)


def unpack(packed, weight_shape, state_shape):
    count = 1
    for size in state_shape[:-1]:
        count *= size
    state = packed[:count].astype(jnp.float32).reshape(state_shape)
    flat = packed[count:].reshape(-1).astype(jnp.float32)
    size = 1
    for s in weight_shape:
        size *= s
    weight = (flat[:size] + flat[size : 2 * size]).reshape(weight_shape)
    return weight, state


def entering_state(weight, state, axis, work=None, work_inputs=()):
    count = lax.axis_size(axis)
    if count == 1:
        return jnp.zeros_like(state), run(work, work_inputs)
    own = pack(weight, state)
    if count == 2:
        return unpack(shifted(own, axis, 1), weight.shape, state.shape)[1], run(work, work_inputs)
    near_w, near_s = unpack(shifted(own, axis, 1), weight.shape, state.shape)
    far_w, far_s = unpack(shifted(own, axis, 2), weight.shape, state.shape)
    state = near_w[..., None, None] * far_s + near_s
    weight = near_w * far_w
    span = 2
    while 2 * span < count:
        far_w, far_s = unpack(shifted(pack(weight, state), axis, span), weight.shape, state.shape)
        state = weight[..., None, None] * far_s + state
        weight = weight * far_w
        span *= 2
    payload = state.astype(jnp.bfloat16)
    if work is not None:
        payload, work_inputs = lax.optimization_barrier((payload, work_inputs))
    far = shifted(payload, axis, span)
    done = run(work, work_inputs)
    if work is not None:
        far, done = lax.optimization_barrier((far, done))
    return weight[..., None, None] * far.astype(jnp.float32) + state, done


def run(work, work_inputs):
    return None if work is None else work(*work_inputs)


def entering_pairs(total, state, lo, hi, work=None, work_inputs=()):
    shape = state.shape
    heads = total.size
    half = heads // 2
    weight = jnp.exp(total).reshape(heads)
    state = state.reshape((heads,) + shape[-2:])
    first = lax.axis_index(lo) == 0
    mine_w = jnp.where(first, weight[:half], weight[half:])
    mine_s = jnp.where(first, state[:half], state[half:])
    other_w = jnp.where(first, weight[half:], weight[:half])
    other_s = jnp.where(first, state[half:], state[:half])
    got_w, got_s = unpack(swap(pack(other_w, other_s), lo), (half,), (half,) + shape[-2:])
    w_first = jnp.where(first, mine_w, got_w)
    s_first = jnp.where(first, mine_s, got_s)
    w_second = jnp.where(first, got_w, mine_w)
    s_second = jnp.where(first, got_s, mine_s)
    pair_w = w_first * w_second
    pair_s = w_second[:, None, None] * s_first + s_second
    at_first, done = entering_state(pair_w, pair_s, hi, work, work_inputs)
    at_second = w_first[:, None, None] * at_first + s_first
    keep = jnp.where(first, at_first, at_second)
    give = jnp.where(first, at_second, at_first)
    got = swap(give.astype(jnp.bfloat16), lo).astype(jnp.float32)
    lower = jnp.where(first, keep, got)
    upper = jnp.where(first, got, keep)
    return jnp.concatenate([lower, upper], axis=0).reshape(shape), done


def body(
    inner_input,
    state_input,
    gate_input,
    step_logits,
    conv_inner,
    conv_states,
    bias_inner,
    bias_states,
    decay_log,
    skip_gain,
    norm_gain,
    out_weight,
):
    tokens = inner_input.shape[0]
    margin = CONV - 1
    inner_width = inner_input.shape[1]
    halo = jnp.concatenate(
        [inner_input[tokens - margin :], state_input[tokens - margin :].reshape(margin, -1)], axis=1
    )
    halo = shifted(halo, ("chi", "clo"), 1)
    inner_conv = jnp.transpose(
        conv_silu_kernel(halo[:, :inner_width], inner_input, conv_inner, bias_inner)
    )
    state_conv = jnp.transpose(
        conv_silu_kernel(
            halo[:, inner_width:],
            state_input.reshape(tokens, -1),
            conv_states.reshape(CONV, -1),
            bias_states.reshape(-1),
        )
    ).reshape(state_input.shape)
    groups_here = state_input.shape[2] // STATE
    per_group = SSM_HEAD_COUNT // GROUPS
    blocks = tokens // BLK
    step_sizes = jax.nn.softplus(step_logits)
    log_rates = -step_sizes * jnp.exp(decay_log)[None]
    c_all = state_conv[:, 1].reshape(blocks, BLK, groups_here, STATE)
    inputs_all = (
        inner_conv.reshape(blocks, BLK, groups_here, per_group, HEAD_DIM),
        state_conv[:, 0].reshape(blocks, BLK, groups_here, STATE),
        c_all,
        step_sizes.reshape(blocks, BLK, groups_here, per_group),
        log_rates.reshape(blocks, BLK, groups_here, per_group),
    )
    if blocks == 1:
        inner_block, b_block, c_block, step_block, rate_block = (x[0] for x in inputs_all)
        cumulative = jnp.cumsum(rate_block, axis=0)
        local_state = state_of(inner_block, b_block, step_block, cumulative)
        state_in, diagonal = entering_pairs(
            cumulative[-1],
            local_state,
            "clo",
            "chi",
            lambda x, b, c: diagonal_of(x, b, c, step_block, cumulative),
            (inner_block, b_block, c_block),
        )
        partial_heads = diagonal[None]
        factors = cumulative[None]
    else:
        start_state = jnp.zeros((groups_here, per_group, HEAD_DIM, STATE), jnp.float32)
        start_total = jnp.zeros((groups_here, per_group), jnp.float32)
        (local_state, device_total), (partial_heads, factors) = lax.scan(
            block_local, (start_state, start_total), inputs_all
        )
        state_in = entering_pairs(device_total, local_state, "clo", "chi")[0]
    correction = jax.vmap(apply_state, in_axes=(0, None, 0))(c_all, state_in, factors)
    width_here = groups_here * per_group * HEAD_DIM
    mixed_heads = (partial_heads + correction).reshape(tokens, width_here) + jnp.repeat(
        skip_gain, HEAD_DIM
    )[None] * inner_conv.astype(jnp.float32)
    gated_out = mixed_heads * jax.nn.silu(gate_input.astype(jnp.float32))
    grouped = gated_out.reshape(tokens, groups_here, width_here // groups_here)
    normed = grouped * lax.rsqrt(jnp.mean(grouped * grouped, axis=-1, keepdims=True) + epsilon)
    normed = (normed.reshape(tokens, width_here) * norm_gain.astype(jnp.float32)).astype(
        jnp.bfloat16
    )
    return reduce_rows(normed, out_weight)


def swap(value, axis):
    return lax.ppermute(value, axis, [(0, 1), (1, 0)])


def reduce_rows(normed, out_weight):
    tokens = normed.shape[0]
    outer = lax.axis_size("ty")
    inner = lax.axis_size("tc")
    piece = tokens // (outer * inner)
    ty = lax.axis_index("ty")
    tc = lax.axis_index("tc")

    def project(block):
        partial = jnp.dot(block, out_weight, preferred_element_type=jnp.float32)
        return partial.astype(jnp.bfloat16)

    if inner != 2:
        projected = project(normed).reshape(outer * inner, piece, -1)
        return lax.psum_scatter(projected, ("ty", "tc"), scatter_dimension=0, tiled=True)[0]
    other = 1 - tc
    width = out_weight.shape[1]
    chunks = 4 if width % (4 * 128) == 0 else 1
    step = width // chunks
    done = []
    payloads = []
    for c in range(chunks):
        source = normed
        if c == chunks - 1 and c > 0 and payloads[0] is not None:
            payloads[0], source = lax.optimization_barrier((payloads[0], normed))
        partial = jnp.dot(
            source, out_weight[:, c * step : (c + 1) * step], preferred_element_type=jnp.float32
        ).astype(jnp.bfloat16)
        partial = partial.reshape(outer, inner, piece, step)
        sent = swap(lax.dynamic_index_in_dim(partial, other, 1, keepdims=False), "tc")
        half = lax.dynamic_index_in_dim(partial, tc, 1, keepdims=False).astype(jnp.float32)
        half = half + sent.astype(jnp.float32)
        if outer == 2:
            payloads.append(
                lax.dynamic_index_in_dim(half, 1 - ty, 0, keepdims=False).astype(jnp.bfloat16)
            )
        else:
            payloads.append(None)
        done.append(half)
    for c in range(chunks):
        half = done[c]
        if outer == 2:
            across = swap(payloads[c], "ty")
            mine = lax.dynamic_index_in_dim(half, ty, 0, keepdims=False)
            done[c] = (mine + across.astype(jnp.float32)).astype(jnp.bfloat16)
        else:
            done[c] = lax.psum_scatter(
                half.astype(jnp.bfloat16), "ty", scatter_dimension=0, tiled=True
            )[0]
    return jnp.concatenate(done, axis=1)


def solution(mesh):
    cores = 2
    split = Mesh(
        mesh.devices.reshape(mesh.shape["ctx"] // 2, 2, mesh.shape["tp"] // cores, cores),
        ("chi", "clo", "ty", "tc"),
    )
    tp = ("ty", "tc")
    ctx = ("chi", "clo")
    placed = (
        P(ctx, tp),
        P(ctx, None, tp),
        P(ctx, tp),
        P(ctx, tp),
        P(None, tp),
        P(None, None, tp),
        P(tp),
        P(None, tp),
        P(tp),
        P(tp),
        P(tp),
        P(tp, None),
    )
    return jax.shard_map(
        body, mesh=split, in_specs=placed, out_specs=P(ctx + tp, None), check_vma=False
    )
```

```python
import jax
import jax.numpy as jnp
from jax import lax
from jax.experimental import pallas as pl
from jax.experimental.pallas import tpu as pltpu
from jax.sharding import Mesh, PartitionSpec as P

SSM_HEAD_COUNT = 128
HEAD_DIM = 64
STATE = 128
GROUPS = 8
CONV = 4
BLK = 512


epsilon = 1e-05


def shifted(value, axis, by):
    names = axis if isinstance(axis, tuple) else (axis,)
    count = 1
    for name in names:
        count *= lax.axis_size(name)
    pairs = [(i, i + by) for i in range(count) if 0 <= i + by < count]
    return lax.ppermute(value, axis, pairs)


def conv_silu(padded, weight, offsets, row_count):
    summed = offsets.astype(jnp.float32)
    for k in range(CONV):
        summed = summed + weight[k].astype(jnp.float32) * padded[k : k + row_count].astype(
            jnp.float32
        )
    return lax.optimization_barrier(jax.nn.silu(summed).astype(jnp.bfloat16))


def conv_kernel(halo_ref, x_ref, w_ref, b_ref, o_ref, pad_ref):
    rows = x_ref.shape[0]
    pad_ref[0:8, :] = halo_ref[...].astype(jnp.float32)
    pad_ref[8 : 8 + rows, :] = x_ref[...].astype(jnp.float32)
    summed = b_ref[...].astype(jnp.float32)
    for k in range(CONV):
        summed = summed + w_ref[k : k + 1, :].astype(jnp.float32) * pad_ref[8 - (CONV - 1) + k : 8 - (CONV - 1) + k + rows, :]
    o_ref[...] = jnp.transpose(jax.nn.silu(summed)).astype(o_ref.dtype)

def conv_silu_kernel(halo, x, weight, bias):
    rows, width = x.shape
    block = 1024 if width % 1024 == 0 else width
    halo8 = jnp.concatenate([jnp.zeros((8 - halo.shape[0], width), halo.dtype), halo], axis=0)
    return pl.pallas_call(
        conv_kernel,
        grid=(width // block,),
        in_specs=[
            pl.BlockSpec((8, block), lambda j: (0, j)),
            pl.BlockSpec((rows, block), lambda j: (0, j)),
            pl.BlockSpec((CONV, block), lambda j: (0, j)),
            pl.BlockSpec((1, block), lambda j: (0, j)),
        ],
        out_specs=pl.BlockSpec((block, rows), lambda j: (j, 0)),
        out_shape=jax.ShapeDtypeStruct((width, rows), jnp.bfloat16),
        scratch_shapes=[pltpu.VMEM((rows + 8, block), jnp.float32)],
    )(halo8, x, weight, bias.reshape(1, width))

def diagonal_of(inner_block, b_block, c_block, step_sizes, cumulative):
    length = inner_block.shape[0]
    along = jnp.transpose(cumulative, (1, 2, 0))
    causal = lax.broadcasted_iota(jnp.int32, (length, length), 0) >= lax.broadcasted_iota(
        jnp.int32, (length, length), 1
    )
    decays = jnp.exp(jnp.where(causal, along[:, :, :, None] - along[:, :, None, :], -jnp.inf))
    scores = jnp.einsum("ign,jgn->gij", c_block, b_block, preferred_element_type=jnp.float32)
    mixing = (
        decays * scores[:, None] * jnp.transpose(step_sizes, (1, 2, 0))[:, :, None, :]
    ).astype(jnp.bfloat16)
    return jnp.einsum("ghij,jghp->ighp", mixing, inner_block, preferred_element_type=jnp.float32)


def state_of(inner_block, b_block, step_sizes, cumulative):
    tail_weight = jnp.exp(cumulative[-1][None] - cumulative) * step_sizes
    weighted = (inner_block * tail_weight[..., None]).astype(jnp.bfloat16)
    return jnp.einsum("jghp,jgn->ghpn", weighted, b_block, preferred_element_type=jnp.float32)


def block_parts(inner_block, b_block, c_block, step_sizes, log_rates):
    cumulative = jnp.cumsum(log_rates, axis=0)
    diagonal = diagonal_of(inner_block, b_block, c_block, step_sizes, cumulative)
    block_state = state_of(inner_block, b_block, step_sizes, cumulative)
    return diagonal, cumulative, block_state


def apply_state(c_block, state, cumulative):
    return jnp.exp(cumulative)[..., None] * jnp.einsum(
        "ign,ghpn->ighp", c_block.astype(jnp.float32), state, precision=lax.Precision.HIGHEST
    )


def block_local(carried_in, inputs_block):
    local_state, entry_total = carried_in
    inner_block, b_block, c_block, step_sizes, log_rates = inputs_block
    diagonal, cumulative, block_state = block_parts(*inputs_block)
    carried = apply_state(c_block, local_state, cumulative)
    new_state = jnp.exp(cumulative[-1])[..., None, None] * local_state + block_state
    return (
        (new_state, entry_total + cumulative[-1]),
        (diagonal + carried, cumulative + entry_total[None]),
    )


def pack(weight, state):
    rows = state.reshape(-1, state.shape[-1])
    high = weight.astype(jnp.bfloat16)
    low = (weight - high.astype(jnp.float32)).astype(jnp.bfloat16)
    lanes = rows.shape[-1]
    flat = jnp.concatenate([high.reshape(-1), low.reshape(-1)])
    pad = (-flat.shape[0]) % (16 * lanes)
    tail = jnp.pad(flat, (0, pad)).reshape(-1, lanes)
    return jnp.concatenate([rows.astype(jnp.bfloat16), tail], axis=0)


def unpack(packed, weight_shape, state_shape):
    count = 1
    for size in state_shape[:-1]:
        count *= size
    state = packed[:count].astype(jnp.float32).reshape(state_shape)
    flat = packed[count:].reshape(-1).astype(jnp.float32)
    size = 1
    for s in weight_shape:
        size *= s
    weight = (flat[:size] + flat[size : 2 * size]).reshape(weight_shape)
    return weight, state


def entering_state(weight, state, axis, work=None, work_inputs=()):
    count = lax.axis_size(axis)
    if count == 1:
        return jnp.zeros_like(state), run(work, work_inputs)
    own = pack(weight, state)
    if count == 2:
        return unpack(shifted(own, axis, 1), weight.shape, state.shape)[1], run(work, work_inputs)
    near_w, near_s = unpack(shifted(own, axis, 1), weight.shape, state.shape)
    far_w, far_s = unpack(shifted(own, axis, 2), weight.shape, state.shape)
    state = near_w[..., None, None] * far_s + near_s
    weight = near_w * far_w
    span = 2
    while 2 * span < count:
        far_w, far_s = unpack(shifted(pack(weight, state), axis, span), weight.shape, state.shape)
        state = weight[..., None, None] * far_s + state
        weight = weight * far_w
        span *= 2
    payload = state.astype(jnp.bfloat16)
    if work is not None:
        payload, work_inputs = lax.optimization_barrier((payload, work_inputs))
    far = shifted(payload, axis, span)
    done = run(work, work_inputs)
    if work is not None:
        far, done = lax.optimization_barrier((far, done))
    return weight[..., None, None] * far.astype(jnp.float32) + state, done


def run(work, work_inputs):
    return None if work is None else work(*work_inputs)


def entering_pairs(total, state, lo, hi, work=None, work_inputs=()):
    shape = state.shape
    heads = total.size
    half = heads // 2
    weight = jnp.exp(total).reshape(heads)
    state = state.reshape((heads,) + shape[-2:])
    first = lax.axis_index(lo) == 0
    mine_w = jnp.where(first, weight[:half], weight[half:])
    mine_s = jnp.where(first, state[:half], state[half:])
    other_w = jnp.where(first, weight[half:], weight[:half])
    other_s = jnp.where(first, state[half:], state[:half])
    got_w, got_s = unpack(swap(pack(other_w, other_s), lo), (half,), (half,) + shape[-2:])
    w_first = jnp.where(first, mine_w, got_w)
    s_first = jnp.where(first, mine_s, got_s)
    w_second = jnp.where(first, got_w, mine_w)
    s_second = jnp.where(first, got_s, mine_s)
    pair_w = w_first * w_second
    pair_s = w_second[:, None, None] * s_first + s_second
    at_first, done = entering_state(pair_w, pair_s, hi, work, work_inputs)
    at_second = w_first[:, None, None] * at_first + s_first
    keep = jnp.where(first, at_first, at_second)
    give = jnp.where(first, at_second, at_first)
    got = swap(give.astype(jnp.bfloat16), lo).astype(jnp.float32)
    lower = jnp.where(first, keep, got)
    upper = jnp.where(first, got, keep)
    return jnp.concatenate([lower, upper], axis=0).reshape(shape), done


def body(
    inner_input,
    state_input,
    gate_input,
    step_logits,
    conv_inner,
    conv_states,
    bias_inner,
    bias_states,
    decay_log,
    skip_gain,
    norm_gain,
    out_weight,
):
    tokens = inner_input.shape[0]
    margin = CONV - 1
    inner_width = inner_input.shape[1]
    halo = jnp.concatenate(
        [inner_input[tokens - margin :], state_input[tokens - margin :].reshape(margin, -1)], axis=1
    )
    halo = shifted(halo, ("chi", "clo"), 1)
    inner_conv = jnp.transpose(
        conv_silu_kernel(halo[:, :inner_width], inner_input, conv_inner, bias_inner)
    )
    state_conv = conv_silu(
        jnp.concatenate([halo[:, inner_width:].reshape((margin,) + state_input.shape[1:]), state_input], axis=0),
        conv_states,
        bias_states,
        tokens,
    )
    groups_here = state_input.shape[2] // STATE
    per_group = SSM_HEAD_COUNT // GROUPS
    blocks = tokens // BLK
    step_sizes = jax.nn.softplus(step_logits)
    log_rates = -step_sizes * jnp.exp(decay_log)[None]
    c_all = state_conv[:, 1].reshape(blocks, BLK, groups_here, STATE)
    inputs_all = (
        inner_conv.reshape(blocks, BLK, groups_here, per_group, HEAD_DIM),
        state_conv[:, 0].reshape(blocks, BLK, groups_here, STATE),
        c_all,
        step_sizes.reshape(blocks, BLK, groups_here, per_group),
        log_rates.reshape(blocks, BLK, groups_here, per_group),
    )
    if blocks == 1:
        inner_block, b_block, c_block, step_block, rate_block = (x[0] for x in inputs_all)
        cumulative = jnp.cumsum(rate_block, axis=0)
        local_state = state_of(inner_block, b_block, step_block, cumulative)
        state_in, diagonal = entering_pairs(
            cumulative[-1],
            local_state,
            "clo",
            "chi",
            lambda x, b, c: diagonal_of(x, b, c, step_block, cumulative),
            (inner_block, b_block, c_block),
        )
        partial_heads = diagonal[None]
        factors = cumulative[None]
    else:
        start_state = jnp.zeros((groups_here, per_group, HEAD_DIM, STATE), jnp.float32)
        start_total = jnp.zeros((groups_here, per_group), jnp.float32)
        (local_state, device_total), (partial_heads, factors) = lax.scan(
            block_local, (start_state, start_total), inputs_all
        )
        state_in = entering_pairs(device_total, local_state, "clo", "chi")[0]
    correction = jax.vmap(apply_state, in_axes=(0, None, 0))(c_all, state_in, factors)
    width_here = groups_here * per_group * HEAD_DIM
    mixed_heads = (partial_heads + correction).reshape(tokens, width_here) + jnp.repeat(
        skip_gain, HEAD_DIM
    )[None] * inner_conv.astype(jnp.float32)
    gated_out = mixed_heads * jax.nn.silu(gate_input.astype(jnp.float32))
    grouped = gated_out.reshape(tokens, groups_here, width_here // groups_here)
    normed = grouped * lax.rsqrt(jnp.mean(grouped * grouped, axis=-1, keepdims=True) + epsilon)
    normed = (normed.reshape(tokens, width_here) * norm_gain.astype(jnp.float32)).astype(
        jnp.bfloat16
    )
    return reduce_rows(normed, out_weight)


def swap(value, axis):
    return lax.ppermute(value, axis, [(0, 1), (1, 0)])


def reduce_rows(normed, out_weight):
    tokens = normed.shape[0]
    outer = lax.axis_size("ty")
    inner = lax.axis_size("tc")
    piece = tokens // (outer * inner)
    ty = lax.axis_index("ty")
    tc = lax.axis_index("tc")

    def project(block):
        partial = jnp.dot(block, out_weight, preferred_element_type=jnp.float32)
        return partial.astype(jnp.bfloat16)

    if inner != 2:
        projected = project(normed).reshape(outer * inner, piece, -1)
        return lax.psum_scatter(projected, ("ty", "tc"), scatter_dimension=0, tiled=True)[0]
    other = 1 - tc
    width = out_weight.shape[1]
    chunks = 4 if width % (4 * 128) == 0 else 1
    step = width // chunks
    done = []
    payloads = []
    for c in range(chunks):
        source = normed
        if c == chunks - 1 and c > 0 and payloads[0] is not None:
            payloads[0], source = lax.optimization_barrier((payloads[0], normed))
        partial = jnp.dot(
            source, out_weight[:, c * step : (c + 1) * step], preferred_element_type=jnp.float32
        ).astype(jnp.bfloat16)
        partial = partial.reshape(outer, inner, piece, step)
        sent = swap(lax.dynamic_index_in_dim(partial, other, 1, keepdims=False), "tc")
        half = lax.dynamic_index_in_dim(partial, tc, 1, keepdims=False).astype(jnp.float32)
        half = half + sent.astype(jnp.float32)
        if outer == 2:
            payloads.append(
                lax.dynamic_index_in_dim(half, 1 - ty, 0, keepdims=False).astype(jnp.bfloat16)
            )
        else:
            payloads.append(None)
        done.append(half)
    for c in range(chunks):
        half = done[c]
        if outer == 2:
            across = swap(payloads[c], "ty")
            mine = lax.dynamic_index_in_dim(half, ty, 0, keepdims=False)
            done[c] = (mine + across.astype(jnp.float32)).astype(jnp.bfloat16)
        else:
            done[c] = lax.psum_scatter(
                half.astype(jnp.bfloat16), "ty", scatter_dimension=0, tiled=True
            )[0]
    return jnp.concatenate(done, axis=1)


def solution(mesh):
    cores = 2
    split = Mesh(
        mesh.devices.reshape(mesh.shape["ctx"] // 2, 2, mesh.shape["tp"] // cores, cores),
        ("chi", "clo", "ty", "tc"),
    )
    tp = ("ty", "tc")
    ctx = ("chi", "clo")
    placed = (
        P(ctx, tp),
        P(ctx, None, tp),
        P(ctx, tp),
        P(ctx, tp),
        P(None, tp),
        P(None, None, tp),
        P(tp),
        P(None, tp),
        P(tp),
        P(tp),
        P(tp),
        P(tp, None),
    )
    return jax.shard_map(
        body, mesh=split, in_specs=placed, out_specs=P(ctx + tp, None), check_vma=False
    )
```

```python
import jax
import jax.numpy as jnp
from jax import lax
from jax.experimental import pallas as pl
from jax.experimental.pallas import tpu as pltpu
from jax.sharding import Mesh, PartitionSpec as P

SSM_HEAD_COUNT = 128
HEAD_DIM = 64
STATE = 128
GROUPS = 8
CONV = 4
BLK = 512


epsilon = 1e-05


def shifted(value, axis, by):
    names = axis if isinstance(axis, tuple) else (axis,)
    count = 1
    for name in names:
        count *= lax.axis_size(name)
    pairs = [(i, i + by) for i in range(count) if 0 <= i + by < count]
    return lax.ppermute(value, axis, pairs)


def conv_silu(padded, weight, offsets, row_count):
    summed = offsets.astype(jnp.float32)
    for k in range(CONV):
        summed = summed + weight[k].astype(jnp.float32) * padded[k : k + row_count].astype(
            jnp.float32
        )
    return lax.optimization_barrier(jax.nn.silu(summed).astype(jnp.bfloat16))


def conv_kernel(halo_ref, x_ref, w_ref, o_ref, pad_ref):
    rows = x_ref.shape[0]
    pad_ref[0:8, :] = halo_ref[...].astype(jnp.float32)
    pad_ref[8 : 8 + rows, :] = x_ref[...].astype(jnp.float32)
    summed = halo_ref[0:1, :].astype(jnp.float32)
    for k in range(CONV):
        summed = summed + w_ref[k : k + 1, :].astype(jnp.float32) * pad_ref[8 - (CONV - 1) + k : 8 - (CONV - 1) + k + rows, :]
    o_ref[...] = jnp.transpose(jax.nn.silu(summed)).astype(o_ref.dtype)

def conv_silu_kernel(halo, x, weight, bias):
    rows, width = x.shape
    block = 512 if width % 512 == 0 else width
    halo8 = jnp.concatenate(
        [bias.reshape(1, width).astype(halo.dtype), jnp.zeros((7 - halo.shape[0], width), halo.dtype), halo],
        axis=0,
    )
    return pl.pallas_call(
        conv_kernel,
        grid=(width // block,),
        in_specs=[
            pl.BlockSpec((8, block), lambda j: (0, j)),
            pl.BlockSpec((rows, block), lambda j: (0, j)),
            pl.BlockSpec((CONV, block), lambda j: (0, j)),
        ],
        out_specs=pl.BlockSpec((block, rows), lambda j: (j, 0)),
        out_shape=jax.ShapeDtypeStruct((width, rows), jnp.bfloat16),
        scratch_shapes=[pltpu.VMEM((rows + 8, block), jnp.float32)],
    )(halo8, x, weight)

def diagonal_of(inner_block, b_block, c_block, step_sizes, cumulative):
    length = inner_block.shape[0]
    along = jnp.transpose(cumulative, (1, 2, 0))
    causal = lax.broadcasted_iota(jnp.int32, (length, length), 0) >= lax.broadcasted_iota(
        jnp.int32, (length, length), 1
    )
    decays = jnp.exp(jnp.where(causal, along[:, :, :, None] - along[:, :, None, :], -jnp.inf))
    scores = jnp.einsum("ign,jgn->gij", c_block, b_block, preferred_element_type=jnp.float32)
    mixing = (
        decays * scores[:, None] * jnp.transpose(step_sizes, (1, 2, 0))[:, :, None, :]
    ).astype(jnp.bfloat16)
    return jnp.einsum("ghij,jghp->ighp", mixing, inner_block, preferred_element_type=jnp.float32)


def state_of(inner_block, b_block, step_sizes, cumulative):
    tail_weight = jnp.exp(cumulative[-1][None] - cumulative) * step_sizes
    weighted = (inner_block * tail_weight[..., None]).astype(jnp.bfloat16)
    return jnp.einsum("jghp,jgn->ghpn", weighted, b_block, preferred_element_type=jnp.float32)


def block_parts(inner_block, b_block, c_block, step_sizes, log_rates):
    cumulative = jnp.cumsum(log_rates, axis=0)
    diagonal = diagonal_of(inner_block, b_block, c_block, step_sizes, cumulative)
    block_state = state_of(inner_block, b_block, step_sizes, cumulative)
    return diagonal, cumulative, block_state


def apply_state(c_block, state, cumulative):
    return jnp.exp(cumulative)[..., None] * jnp.einsum(
        "ign,ghpn->ighp", c_block.astype(jnp.float32), state, precision=lax.Precision.HIGHEST
    )


def block_local(carried_in, inputs_block):
    local_state, entry_total = carried_in
    inner_block, b_block, c_block, step_sizes, log_rates = inputs_block
    diagonal, cumulative, block_state = block_parts(*inputs_block)
    carried = apply_state(c_block, local_state, cumulative)
    new_state = jnp.exp(cumulative[-1])[..., None, None] * local_state + block_state
    return (
        (new_state, entry_total + cumulative[-1]),
        (diagonal + carried, cumulative + entry_total[None]),
    )


def pack(weight, state):
    rows = state.reshape(-1, state.shape[-1])
    high = weight.astype(jnp.bfloat16)
    low = (weight - high.astype(jnp.float32)).astype(jnp.bfloat16)
    lanes = rows.shape[-1]
    flat = jnp.concatenate([high.reshape(-1), low.reshape(-1)])
    pad = (-flat.shape[0]) % (16 * lanes)
    tail = jnp.pad(flat, (0, pad)).reshape(-1, lanes)
    return jnp.concatenate([rows.astype(jnp.bfloat16), tail], axis=0)


def unpack(packed, weight_shape, state_shape):
    count = 1
    for size in state_shape[:-1]:
        count *= size
    state = packed[:count].astype(jnp.float32).reshape(state_shape)
    flat = packed[count:].reshape(-1).astype(jnp.float32)
    size = 1
    for s in weight_shape:
        size *= s
    weight = (flat[:size] + flat[size : 2 * size]).reshape(weight_shape)
    return weight, state


def entering_state(weight, state, axis, work=None, work_inputs=()):
    count = lax.axis_size(axis)
    if count == 1:
        return jnp.zeros_like(state), run(work, work_inputs)
    own = pack(weight, state)
    if count == 2:
        return unpack(shifted(own, axis, 1), weight.shape, state.shape)[1], run(work, work_inputs)
    near_w, near_s = unpack(shifted(own, axis, 1), weight.shape, state.shape)
    far_w, far_s = unpack(shifted(own, axis, 2), weight.shape, state.shape)
    state = near_w[..., None, None] * far_s + near_s
    weight = near_w * far_w
    span = 2
    while 2 * span < count:
        far_w, far_s = unpack(shifted(pack(weight, state), axis, span), weight.shape, state.shape)
        state = weight[..., None, None] * far_s + state
        weight = weight * far_w
        span *= 2
    payload = state.astype(jnp.bfloat16)
    if work is not None:
        payload, work_inputs = lax.optimization_barrier((payload, work_inputs))
    far = shifted(payload, axis, span)
    done = run(work, work_inputs)
    if work is not None:
        far, done = lax.optimization_barrier((far, done))
    return weight[..., None, None] * far.astype(jnp.float32) + state, done


def run(work, work_inputs):
    return None if work is None else work(*work_inputs)


def entering_pairs(total, state, lo, hi, work=None, work_inputs=()):
    shape = state.shape
    heads = total.size
    half = heads // 2
    weight = jnp.exp(total).reshape(heads)
    state = state.reshape((heads,) + shape[-2:])
    first = lax.axis_index(lo) == 0
    mine_w = jnp.where(first, weight[:half], weight[half:])
    mine_s = jnp.where(first, state[:half], state[half:])
    other_w = jnp.where(first, weight[half:], weight[:half])
    other_s = jnp.where(first, state[half:], state[:half])
    got_w, got_s = unpack(swap(pack(other_w, other_s), lo), (half,), (half,) + shape[-2:])
    w_first = jnp.where(first, mine_w, got_w)
    s_first = jnp.where(first, mine_s, got_s)
    w_second = jnp.where(first, got_w, mine_w)
    s_second = jnp.where(first, got_s, mine_s)
    pair_w = w_first * w_second
    pair_s = w_second[:, None, None] * s_first + s_second
    at_first, done = entering_state(pair_w, pair_s, hi, work, work_inputs)
    at_second = w_first[:, None, None] * at_first + s_first
    keep = jnp.where(first, at_first, at_second)
    give = jnp.where(first, at_second, at_first)
    got = swap(give.astype(jnp.bfloat16), lo).astype(jnp.float32)
    lower = jnp.where(first, keep, got)
    upper = jnp.where(first, got, keep)
    return jnp.concatenate([lower, upper], axis=0).reshape(shape), done


def body(
    inner_input,
    state_input,
    gate_input,
    step_logits,
    conv_inner,
    conv_states,
    bias_inner,
    bias_states,
    decay_log,
    skip_gain,
    norm_gain,
    out_weight,
):
    tokens = inner_input.shape[0]
    margin = CONV - 1
    inner_width = inner_input.shape[1]
    halo = jnp.concatenate(
        [inner_input[tokens - margin :], state_input[tokens - margin :].reshape(margin, -1)], axis=1
    )
    halo = shifted(halo, ("chi", "clo"), 1)
    inner_conv = jnp.transpose(
        conv_silu_kernel(halo[:, :inner_width], inner_input, conv_inner, bias_inner)
    )
    state_conv = conv_silu(
        jnp.concatenate([halo[:, inner_width:].reshape((margin,) + state_input.shape[1:]), state_input], axis=0),
        conv_states,
        bias_states,
        tokens,
    )
    groups_here = state_input.shape[2] // STATE
    per_group = SSM_HEAD_COUNT // GROUPS
    blocks = tokens // BLK
    step_sizes = jax.nn.softplus(step_logits)
    log_rates = -step_sizes * jnp.exp(decay_log)[None]
    c_all = state_conv[:, 1].reshape(blocks, BLK, groups_here, STATE)
    inputs_all = (
        inner_conv.reshape(blocks, BLK, groups_here, per_group, HEAD_DIM),
        state_conv[:, 0].reshape(blocks, BLK, groups_here, STATE),
        c_all,
        step_sizes.reshape(blocks, BLK, groups_here, per_group),
        log_rates.reshape(blocks, BLK, groups_here, per_group),
    )
    if blocks == 1:
        inner_block, b_block, c_block, step_block, rate_block = (x[0] for x in inputs_all)
        cumulative = jnp.cumsum(rate_block, axis=0)
        local_state = state_of(inner_block, b_block, step_block, cumulative)
        state_in, diagonal = entering_pairs(
            cumulative[-1],
            local_state,
            "clo",
            "chi",
            lambda x, b, c: diagonal_of(x, b, c, step_block, cumulative),
            (inner_block, b_block, c_block),
        )
        partial_heads = diagonal[None]
        factors = cumulative[None]
    else:
        start_state = jnp.zeros((groups_here, per_group, HEAD_DIM, STATE), jnp.float32)
        start_total = jnp.zeros((groups_here, per_group), jnp.float32)
        (local_state, device_total), (partial_heads, factors) = lax.scan(
            block_local, (start_state, start_total), inputs_all
        )
        state_in = entering_pairs(device_total, local_state, "clo", "chi")[0]
    correction = jax.vmap(apply_state, in_axes=(0, None, 0))(c_all, state_in, factors)
    width_here = groups_here * per_group * HEAD_DIM
    mixed_heads = (partial_heads + correction).reshape(tokens, width_here) + jnp.repeat(
        skip_gain, HEAD_DIM
    )[None] * inner_conv.astype(jnp.float32)
    gated_out = mixed_heads * jax.nn.silu(gate_input.astype(jnp.float32))
    grouped = gated_out.reshape(tokens, groups_here, width_here // groups_here)
    normed = grouped * lax.rsqrt(jnp.mean(grouped * grouped, axis=-1, keepdims=True) + epsilon)
    normed = (normed.reshape(tokens, width_here) * norm_gain.astype(jnp.float32)).astype(
        jnp.bfloat16
    )
    return reduce_rows(normed, out_weight)


def swap(value, axis):
    return lax.ppermute(value, axis, [(0, 1), (1, 0)])


def reduce_rows(normed, out_weight):
    tokens = normed.shape[0]
    outer = lax.axis_size("ty")
    inner = lax.axis_size("tc")
    piece = tokens // (outer * inner)
    ty = lax.axis_index("ty")
    tc = lax.axis_index("tc")

    def project(block):
        partial = jnp.dot(block, out_weight, preferred_element_type=jnp.float32)
        return partial.astype(jnp.bfloat16)

    if inner != 2:
        projected = project(normed).reshape(outer * inner, piece, -1)
        return lax.psum_scatter(projected, ("ty", "tc"), scatter_dimension=0, tiled=True)[0]
    other = 1 - tc
    width = out_weight.shape[1]
    chunks = 4 if width % (4 * 128) == 0 else 1
    step = width // chunks
    done = []
    payloads = []
    for c in range(chunks):
        source = normed
        if c == chunks - 1 and c > 0 and payloads[0] is not None:
            payloads[0], source = lax.optimization_barrier((payloads[0], normed))
        partial = jnp.dot(
            source, out_weight[:, c * step : (c + 1) * step], preferred_element_type=jnp.float32
        ).astype(jnp.bfloat16)
        partial = partial.reshape(outer, inner, piece, step)
        sent = swap(lax.dynamic_index_in_dim(partial, other, 1, keepdims=False), "tc")
        half = lax.dynamic_index_in_dim(partial, tc, 1, keepdims=False).astype(jnp.float32)
        half = half + sent.astype(jnp.float32)
        if outer == 2:
            payloads.append(
                lax.dynamic_index_in_dim(half, 1 - ty, 0, keepdims=False).astype(jnp.bfloat16)
            )
        else:
            payloads.append(None)
        done.append(half)
    for c in range(chunks):
        half = done[c]
        if outer == 2:
            across = swap(payloads[c], "ty")
            mine = lax.dynamic_index_in_dim(half, ty, 0, keepdims=False)
            done[c] = (mine + across.astype(jnp.float32)).astype(jnp.bfloat16)
        else:
            done[c] = lax.psum_scatter(
                half.astype(jnp.bfloat16), "ty", scatter_dimension=0, tiled=True
            )[0]
    return jnp.concatenate(done, axis=1)


def solution(mesh):
    cores = 2
    split = Mesh(
        mesh.devices.reshape(mesh.shape["ctx"] // 2, 2, mesh.shape["tp"] // cores, cores),
        ("chi", "clo", "ty", "tc"),
    )
    tp = ("ty", "tc")
    ctx = ("chi", "clo")
    placed = (
        P(ctx, tp),
        P(ctx, None, tp),
        P(ctx, tp),
        P(ctx, tp),
        P(None, tp),
        P(None, None, tp),
        P(tp),
        P(None, tp),
        P(tp),
        P(tp),
        P(tp),
        P(tp, None),
    )
    return jax.shard_map(
        body, mesh=split, in_specs=placed, out_specs=P(ctx + tp, None), check_vma=False
    )
```
